32 devices in a mesh: dp: 8 (over z, y), tensor: 4 (over x, core).
Axes of the slice: x: 2, y: 2, z: 4, core: 2. Of those that a mesh axis runs over, the one named last changes fastest.
Arguments:
- hidden_in: bfloat16 [4096, 1024], P(('dp', 'tensor')), may hold values from -6 to 6
- cotangent: bfloat16 [4096, 1024], P(('dp', 'tensor')), may hold values from -6 to 6
- segment_ids: int32 [8, 512], P('dp'), may hold values from 0 to 3, never falling along the last dimension, each value on 1 to 256 neighbouring positions
- live_count: int32 [8], P('dp'), may hold values from 256 to 512, as said below
- first_gain: bfloat16 [1024], P(('dp', 'tensor')), may hold values from 0.25 to 1.75
- first_bias: bfloat16 [1024], P(('dp', 'tensor')), may hold values from -3 to 3
- second_gain: bfloat16 [1024], P(('dp', 'tensor')), may hold values from 0.25 to 1.75
- second_bias: bfloat16 [1024], P(('dp', 'tensor')), may hold values from -3 to 3
- attend_weight: bfloat16 [1024, 3, 1024], P('dp', None, 'tensor'), may hold values from -0.1875 to 0.1875
- attend_bias: bfloat16 [3, 1024], P(None, ('tensor', 'dp')), may hold values from -3 to 3
- output_weight: bfloat16 [1024, 1024], P('tensor', 'dp'), may hold values from -0.75 to 0.75
- output_bias: bfloat16 [1024], P(('dp', 'tensor')), may hold values from -3 to 3
- expand_weight: bfloat16 [1024, 4096], P('dp', 'tensor'), may hold values from -0.1875 to 0.1875
- expand_bias: bfloat16 [4096], P(('tensor', 'dp')), may hold values from -3 to 3
- shrink_weight: bfloat16 [4096, 1024], P('tensor', 'dp'), may hold values from -0.09375 to 0.09375
- shrink_bias: bfloat16 [1024], P(('dp', 'tensor')), may hold values from -3 to 3
Outputs:
- hidden_out: bfloat16 [4096, 1024], P(('dp', 'tensor'))
- input_grad: float32 [4096, 1024], P(('dp', 'tensor'))
- first_gain_grad: float32 [1024], P(('dp', 'tensor'))
- first_bias_grad: float32 [1024], P(('dp', 'tensor'))
- second_gain_grad: float32 [1024], P(('dp', 'tensor'))
- second_bias_grad: float32 [1024], P(('dp', 'tensor'))
- attend_weight_grad: float32 [1024, 3, 1024], P('dp', None, 'tensor')
- attend_bias_grad: float32 [3, 1024], P(None, ('tensor', 'dp'))
- output_weight_grad: float32 [1024, 1024], P('tensor', 'dp')
- output_bias_grad: float32 [1024], P(('dp', 'tensor'))
- expand_weight_grad: float32 [1024, 4096], P('dp', 'tensor')
- expand_bias_grad: float32 [4096], P(('tensor', 'dp'))
- shrink_weight_grad: float32 [4096, 1024], P('tensor', 'dp')
- shrink_bias_grad: float32 [1024], P(('dp', 'tensor'))
The draws below stay inside these ranges and needn't reach their ends.
Inputs may be any that keep to these rules, and one draw needn't show every extreme that they name: `segment_ids`: in each group the segment ids never fall; each sequence has 1 to 256 tokens, and one has exactly 256. `live_count`: some group has all 512 tokens live.
All inputs are finite; a program needn't handle non-finite values.
Results may differ from the reference program's by a relative error of at most 0.012.
Values may be sent and summed in bfloat16 or wider, within the bound.
No kernel may reach another device: no remote copies, remote signals or barrier semaphores. Data moves between devices by JAX's collectives and lax.ppermute only.
A program may use at most 128 MiB of HBM per device.

```python
import math
import jax
import jax.numpy as jnp
import numpy as np
from jax import lax

D = 1024
HEADS = 16
HD = 64
FF = 4096
ROT = 16
GROUP_TOK = 512
GROUPS = 8
TOKENS = 4096
SEGS = 4
LONGEST = 256


def draw_live_count(key, part):
    base_counts = jax.random.randint(jax.random.fold_in(key, 11), (GROUPS,), GROUP_TOK // 2, GROUP_TOK + 1)
    chosen = jax.random.randint(jax.random.fold_in(key, 12), (), 0, GROUPS)
    return jnp.where(jnp.arange(GROUPS) == chosen, GROUP_TOK, base_counts).astype(jnp.int32)


def raised(entries, own_key, source, target, shards_of, factor):
    owner, partner = [(jnp.arange(entries.shape[dim]) // (entries.shape[dim] // shards_of)).reshape([-1 if axis == dim else 1 for axis in range(entries.ndim)]) for dim in (source, target)]
    chosen = jax.random.permutation(own_key, shards_of)[partner]
    strong = (owner == chosen) | (owner == (partner + shards_of // 2) % shards_of)
    return jnp.where(strong, factor * entries, entries)


def shard_levels(own_key, dims, split, low, high):
    def one(axis_at, parts):
        steps = jax.random.uniform(jax.random.fold_in(jax.random.fold_in(own_key, 6), axis_at), (parts,), jnp.float32, low / len(split), high / len(split))
        return jnp.repeat(jnp.exp(steps), dims[axis_at] // parts).reshape((-1,) + (1,) * (len(dims) - axis_at - 1))

    level = one(*split[0])
    for cut in split[1:]:
        level = level * one(*cut)
    return level


def profile(amount, total, reach, skew):
    weights = [(1 << 20) // math.isqrt(rank ** skew) + 1 for rank in range(2, amount + 1)]
    rest, given = total - reach - (amount - 1), [1] * (amount - 1)
    while rest > 0:
        free = [i for i in range(amount - 1) if given[i] < reach]
        whole, left = sum([weights[i] for i in free]), rest
        for i in free:
            extra = min(reach - given[i], max(1, left * weights[i] // whole), rest)
            given[i] = given[i] + extra
            rest = rest - extra
    return np.array([reach] + given)


def uneven_parts(rng, number_of, total, limit, slope):
    if number_of == 2:
        one = jax.random.randint(rng, (), max(1, total - limit), min(limit, total - 1) + 1)
        return jnp.stack([one, total - one])
    sizes = jnp.asarray(profile(number_of, total, limit, slope), jnp.int32)
    couples = (number_of - 1) // 2
    donor, taker = sizes[1:1 + 2 * couples:2], sizes[2:2 + 2 * couples:2]
    slack = jnp.minimum(donor - 1, limit - taker)
    shifted = jax.random.randint(jax.random.fold_in(rng, 1), (couples,), 0, 1 << 20) % (slack + 1)
    sizes = sizes.at[1:1 + 2 * couples:2].set(donor - shifted).at[2:2 + 2 * couples:2].set(taker + shifted)
    return sizes[jax.random.permutation(jax.random.fold_in(rng, 2), number_of)]


def normal_values(key, extent, deviation, most, pieces=(), kind=jnp.bfloat16):
    drawn = deviation * jax.random.normal(key, extent, jnp.float32)
    if pieces:
        drawn = drawn * shard_levels(key, extent, pieces, -0.22, 0.18)
    return jnp.clip(drawn, -most, most).astype(kind)


def noise_with(stream_key, shape, width, most, split, heavy, held_as=jnp.bfloat16):
    result = width * jax.random.normal(stream_key, shape, jnp.float32)
    if split:
        result = result * shard_levels(stream_key, shape, split, -0.22, 0.18)
    return jnp.clip(raised(result, jax.random.fold_in(stream_key, 3), *heavy), -most, most).astype(held_as)


def setup_inputs(seed: int = 0) -> dict:
    key_of = jax.random.split(jax.random.key(seed), 17)
    return {
        "hidden_in": normal_values(key_of[0], (TOKENS, D), 1.0, 6.0, ((0, 32),)),
        "cotangent": noise_with(key_of[1], (TOKENS, D), 1.0, 6.0, ((0, 32),), (0, 1, 32, 2.75)),
        "segment_ids": jax.vmap(lambda own: jnp.searchsorted(jnp.cumsum(uneven_parts(own, SEGS, GROUP_TOK, LONGEST, 0)), jnp.arange(GROUP_TOK), side="right"))(jax.random.split(key_of[2], GROUPS)).reshape((GROUPS, GROUP_TOK)).astype(jnp.int32),
        "live_count": draw_live_count(jax.random.fold_in(key_of[16], 71), 0),
        "first_gain": jnp.clip(1.0 + 0.15 * jax.random.normal(key_of[4], (D,), jnp.float32), 0.25, 1.75).astype(jnp.bfloat16),
        "first_bias": normal_values(key_of[5], (D,), 0.5, 3.0, ((0, 32),)),
        "second_gain": jnp.clip(1.0 + 0.15 * jax.random.normal(key_of[6], (D,), jnp.float32), 0.25, 1.75).astype(jnp.bfloat16),
        "second_bias": normal_values(key_of[7], (D,), 0.5, 3.0, ((0, 32),)),
        "attend_weight": normal_values(key_of[8], (D, 3, D), D ** -0.5, 0.1875, ((0, 8), (2, 4))),
        "attend_bias": normal_values(key_of[9], (3, D), 0.5, 3.0, ((1, 32),)),
        "output_weight": normal_values(key_of[10], (D, D), (D // 16) ** -0.5, 0.75, ((0, 4), (1, 8))),
        "output_bias": normal_values(key_of[11], (D,), 0.5, 3.0, ((0, 32),)),
        "expand_weight": normal_values(key_of[12], (D, FF), D ** -0.5, 0.1875, ((0, 8), (1, 4))),
        "expand_bias": normal_values(key_of[13], (FF,), 0.5, 3.0, ((0, 32),)),
        "shrink_weight": normal_values(key_of[14], (FF, D), FF ** -0.5, 0.09375, ((0, 4), (1, 8))),
        "shrink_bias": normal_values(key_of[15], (D,), 0.5, 3.0, ((0, 32),)),
    }


EPSILON = 1e-05
HIGHEST = lax.Precision.HIGHEST

@jax.custom_vjp
def low(v):
    return lax.optimization_barrier(v.astype(jnp.bfloat16)).astype(jnp.float32)

@jax.custom_vjp
def low_back(v):
    return v

def low_keep(v):
    return (low(v), None)

def low_pass(kept, grad):
    return (grad,)

def back_keep(v):
    return (v, None)

def back_low(kept, grad):
    return (low(grad),)
low.defvjp(low_keep, low_pass)
low_back.defvjp(back_keep, back_low)

def normalize(values, gain, shift):
    centre = values - lax.optimization_barrier(jnp.mean(values, axis=-1, keepdims=True))
    variance = lax.optimization_barrier(jnp.mean(centre * centre, axis=-1, keepdims=True))
    return centre * lax.rsqrt(variance + EPSILON) * gain + shift

def rotate(tensor, cos_table, sin_table):
    half_dims = ROT // 2
    lower_half = tensor[..., :half_dims]
    upper_half = tensor[..., half_dims:ROT]
    return jnp.concatenate([lower_half * cos_table - upper_half * sin_table, upper_half * cos_table + lower_half * sin_table, tensor[..., ROT:]], axis=-1)

def group_layer(rows, segments, live, params):
    first_gain, first_bias, second_gain, second_bias, attend_weight, attend_bias, output_weight, output_bias, expand_weight, expand_bias, shrink_weight, shrink_bias = params
    count = rows.shape[0]
    index = jnp.arange(count)
    same_seq = segments[:, None] == segments[None, :]
    positions = lax.optimization_barrier(jnp.sum((same_seq & (index[None, :] < index[:, None])).astype(jnp.float32), axis=1))
    allowed = same_seq & (index[None, :] <= index[:, None]) & ((index[None, :] < live) | (index[None, :] == index[:, None]))
    branch_one = low(normalize(rows, first_gain, first_bias))
    branch_two = low(normalize(rows, second_gain, second_bias))
    projected = low_back(jnp.einsum('td,dcn->tcn', branch_one, attend_weight, precision=HIGHEST) + attend_bias[None])
    per_head = projected.reshape(count, 3, HEADS, HD)
    half_dims = ROT // 2
    inverse = 10000.0 ** (-jnp.arange(half_dims).astype(jnp.float32) * 2.0 / ROT)
    angles = positions[:, None] * inverse[None, :]
    cos_table = jnp.cos(angles)[:, None, :]
    sin_table = jnp.sin(angles)[:, None, :]
    queries = low(rotate(per_head[:, 0], cos_table, sin_table))
    keys_rot = low(rotate(per_head[:, 1], cos_table, sin_table))
    values = low(per_head[:, 2])
    scores = low_back(jnp.einsum('thd,uhd->htu', queries, keys_rot, precision=HIGHEST) * HD ** (-0.5))
    scores = jnp.where(allowed[None], scores, -1000000000.0)
    probs = low(jax.nn.softmax(scores, axis=-1))
    mixed = jnp.einsum('htu,uhd->thd', probs, values, precision=HIGHEST).reshape(count, D)
    mixed = low_back(low(mixed))
    attended = jnp.dot(mixed, output_weight, precision=HIGHEST) + output_bias
    expanded = low_back(jnp.dot(branch_two, expand_weight, precision=HIGHEST) + expand_bias)
    activated = low(jax.nn.gelu(expanded, approximate=False))
    return rows + attended + jnp.dot(activated, shrink_weight, precision=HIGHEST) + shrink_bias

def reference(hidden_in, cotangent, segment_ids, live_count, first_gain, first_bias, second_gain, second_bias, attend_weight, attend_bias, output_weight, output_bias, expand_weight, expand_bias, shrink_weight, shrink_bias):
    floats = [item.astype(jnp.float32) for item in (hidden_in, first_gain, first_bias, second_gain, second_bias, attend_weight, attend_bias, output_weight, output_bias, expand_weight, expand_bias, shrink_weight, shrink_bias)]

    def forward(rows_all, *params):
        blocks = rows_all.reshape(GROUPS, GROUP_TOK, D)

        def one_group(item):
            rows, segments, live = item
            return group_layer(rows, segments, live, params)
        return lax.map(jax.checkpoint(one_group), (blocks, segment_ids, live_count)).reshape(TOKENS, D)
    hidden_out, pullback = jax.vjp(forward, *floats)
    grads = pullback(cotangent.astype(jnp.float32))
    return (hidden_out.astype(jnp.bfloat16), grads[0], grads[1], grads[2], grads[3], grads[4], grads[5], grads[6], grads[7], grads[8], grads[9], grads[10], grads[11], grads[12])
```

```python
import jax
import jax.numpy as jnp
from jax import lax
from jax.sharding import PartitionSpec as P

HD = 64
ROT = 16


EPSILON = 1e-05
NEGATIVE = -1000000000.0


def rotate(tensor, cos_table, sin_table, rot_dims):
    half_dims = rot_dims // 2
    lower_half = tensor[..., :half_dims]
    upper_half = tensor[..., half_dims:rot_dims]
    return jnp.concatenate(
        [
            lower_half * cos_table - upper_half * sin_table,
            upper_half * cos_table + lower_half * sin_table,
            tensor[..., rot_dims:],
        ],
        axis=-1,
    )


def norm_backward(scaled, standard, inverse_std):
    mean_scaled = jnp.mean(scaled, axis=-1, keepdims=True)
    mean_cross = jnp.mean(scaled * standard, axis=-1, keepdims=True)
    return inverse_std * (scaled - mean_scaled - standard * mean_cross)


def lane_rows(parts, axis=1):
    padded = []
    for part in parts:
        extra = -part.shape[1] % 128
        padded.append(jnp.pad(part, ((0, 0), (0, extra))))
    joined = jnp.concatenate(padded, axis=axis)
    joined = joined.reshape(joined.shape[0], -1, 128)
    joined = jnp.pad(joined, ((0, 0), (0, -joined.shape[1] % 16), (0, 0)))
    return joined.reshape(-1, 128)


def solution(mesh):
    dp_count = mesh.shape["dp"]
    tp_count = mesh.shape["tensor"]

    def per_device(
        hidden_in,
        cotangent,
        segment_ids,
        live_count,
        first_gain,
        first_bias,
        second_gain,
        second_bias,
        attend_weight,
        attend_bias,
        output_weight,
        output_bias,
        expand_weight,
        expand_bias,
        shrink_weight,
        shrink_bias,
    ):
        f32 = jnp.float32
        bf16 = jnp.bfloat16
        local_rows, width = hidden_in.shape
        group_rows = local_rows * tp_count
        piece = first_gain.shape[0]
        dp_rows, _, local_cols = attend_weight.shape
        local_ff = expand_weight.shape[1]
        tensor_index = lax.axis_index("tensor")

        small = jnp.concatenate(
            [
                first_gain,
                first_bias,
                second_gain,
                second_bias,
                output_bias,
                shrink_bias,
                attend_bias.reshape(-1),
                expand_bias,
            ]
        )
        small_len = small.shape[0]
        small_row = jnp.zeros((1, width), bf16).at[0, :small_len].set(small)
        gathered = lax.all_gather(
            jnp.concatenate([hidden_in, cotangent, small_row], axis=0), "tensor", axis=0
        )
        rows_all = gathered[:, :local_rows].reshape(group_rows, width)
        grad_rows = gathered[:, local_rows : 2 * local_rows].reshape(group_rows, width)
        small_tensor = gathered[:, 2 * local_rows, :small_len]

        ffn_sizes = (expand_weight.size, shrink_weight.size)
        ffn_all = lax.all_gather(
            jnp.concatenate(
                [expand_weight.reshape(-1), shrink_weight.reshape(-1), small_tensor.reshape(-1)]
            ),
            "dp",
            axis=0,
        )
        expand_full = ffn_all[:, : ffn_sizes[0]].reshape(dp_count * dp_rows, local_ff)
        shrink_parts = ffn_all[:, ffn_sizes[0] : ffn_sizes[0] + ffn_sizes[1]].reshape(
            dp_count, local_ff, dp_rows
        )
        small_all = ffn_all[:, ffn_sizes[0] + ffn_sizes[1] :].reshape(dp_count, tp_count, small_len)

        def full_vector(k):
            return small_all[:, :, k * piece : (k + 1) * piece].reshape(-1).astype(f32)

        gain_one, bias_one, gain_two, bias_two, out_bias_full, shrink_bias_full = [
            full_vector(k) for k in range(6)
        ]
        small_mine = lax.dynamic_index_in_dim(small_all, tensor_index, axis=1, keepdims=False)
        attend_bias_full = (
            small_mine[:, 6 * piece : 6 * piece + attend_bias.size]
            .reshape(dp_count, 3, attend_bias.shape[1])
            .transpose(1, 0, 2)
            .reshape(3, local_cols)
        )
        expand_bias_full = small_mine[:, 6 * piece + attend_bias.size :].reshape(-1)

        attend_all = lax.all_gather(
            jnp.concatenate([attend_weight.reshape(-1), output_weight.reshape(-1)]), "dp", axis=0
        )
        attend_full = attend_all[:, : attend_weight.size].reshape(dp_count * dp_rows, 3, local_cols)
        output_parts = attend_all[:, attend_weight.size :].reshape(dp_count, local_cols, dp_rows)

        local_heads = local_cols // HD
        scale = HD ** (-0.5)
        rows_float = rows_all.astype(f32)
        centre = rows_float - jnp.mean(rows_float, axis=-1, keepdims=True)
        inverse_std = lax.rsqrt(jnp.mean(centre * centre, axis=-1, keepdims=True) + EPSILON)
        standard = centre * inverse_std
        branch_one = (standard * gain_one + bias_one).astype(bf16)
        branch_two = (standard * gain_two + bias_two).astype(bf16)
        grad_rows_parts = grad_rows.reshape(group_rows, dp_count, dp_rows)

        expanded = jnp.dot(
            branch_two, expand_full, preferred_element_type=f32
        ) + expand_bias_full.astype(f32)
        activated, gelu_back = jax.vjp(lambda value: jax.nn.gelu(value, approximate=False), expanded)
        activated_low = activated.astype(bf16)
        ffn_out = jnp.einsum(
            "tf,kfe->tke", activated_low, shrink_parts, preferred_element_type=f32
        ).reshape(group_rows, width)
        grad_activated = jnp.einsum(
            "tke,kfe->tf", grad_rows_parts, shrink_parts, preferred_element_type=f32
        )
        shrink_grad = jnp.einsum(
            "tf,tke->kfe", activated_low, grad_rows_parts, preferred_element_type=f32
        )
        grad_expanded = gelu_back(grad_activated)[0].astype(bf16)
        expand_bias_grad = jnp.sum(grad_expanded.astype(f32), axis=0)
        expand_grad = jnp.einsum("td,tf->df", branch_two, grad_expanded, preferred_element_type=f32)
        grad_two = jnp.einsum("tf,df->td", grad_expanded, expand_full, preferred_element_type=f32)
        out_bias_sum = jnp.sum(grad_rows.astype(f32), axis=0).reshape(dp_count, tp_count, piece)
        out_bias_mine = lax.dynamic_index_in_dim(out_bias_sum, tensor_index, axis=1, keepdims=False)
        ffn_grads = lax.psum_scatter(
            lane_rows(
                [
                    expand_grad.reshape(dp_count, -1),
                    shrink_grad.reshape(dp_count, -1),
                    expand_bias_grad.reshape(dp_count, -1),
                    out_bias_mine,
                ],
                axis=1,
            ).astype(bf16),
            "dp",
            scatter_dimension=0,
            tiled=True,
        ).reshape(-1).astype(f32)
        at = 0
        expand_weight_grad = ffn_grads[at : at + expand_weight.size].reshape(expand_weight.shape)
        at += -(-expand_weight.size // 128) * 128
        shrink_weight_grad = ffn_grads[at : at + shrink_weight.size].reshape(shrink_weight.shape)
        at += -(-shrink_weight.size // 128) * 128
        expand_bias_out = ffn_grads[at : at + expand_bias.size]
        at += -(-expand_bias.size // 128) * 128
        out_bias_grad = ffn_grads[at : at + piece]

        projected = (
            jnp.einsum("td,dcn->tcn", branch_one, attend_full, preferred_element_type=f32)
            + attend_bias_full.astype(f32)[None]
        )
        segments = segment_ids[0]
        index = jnp.arange(group_rows)
        same_seq = segments[:, None] == segments[None, :]
        positions = jnp.sum((same_seq & (index[None, :] < index[:, None])).astype(f32), axis=1)
        allowed = (
            same_seq
            & (index[None, :] <= index[:, None])
            & ((index[None, :] < live_count[0]) | (index[None, :] == index[:, None]))
        )
        half_dims = ROT // 2
        inverse = 10000.0 ** (-jnp.arange(half_dims).astype(f32) * 2.0 / ROT)
        angles = positions[:, None] * inverse[None, :]
        cos_table = jnp.cos(angles)[:, None, :]
        sin_table = jnp.sin(angles)[:, None, :]
        per_head = projected.reshape(group_rows, 3, local_heads, HD)
        queries = rotate(per_head[:, 0], cos_table, sin_table, ROT).astype(bf16)
        keys_rot = rotate(per_head[:, 1], cos_table, sin_table, ROT).astype(bf16)
        values = per_head[:, 2].astype(bf16)
        scores = jnp.einsum("thd,uhd->htu", queries, keys_rot, preferred_element_type=f32) * scale
        scores = jnp.where(allowed[None], scores, NEGATIVE)
        top_score = jnp.max(scores, axis=-1, keepdims=True)
        log_total = top_score + jnp.log(jnp.sum(jnp.exp(scores - top_score), axis=-1, keepdims=True))
        probs = jnp.exp(scores - log_total)
        mixed = jnp.einsum("htu,uhd->thd", probs.astype(bf16), values, preferred_element_type=f32)
        mixed = mixed.reshape(group_rows, local_heads * HD).astype(bf16)
        partial_out = ffn_out + jnp.einsum(
            "tn,kne->tke", mixed, output_parts, preferred_element_type=f32
        ).reshape(group_rows, width)

        grad_mixed = jnp.einsum(
            "tke,kne->tn", grad_rows_parts, output_parts, preferred_element_type=f32
        ).astype(bf16)
        output_grad = jnp.einsum("tn,tke->kne", mixed, grad_rows_parts, preferred_element_type=f32)
        grad_mixed = grad_mixed.reshape(group_rows, local_heads, HD)
        probs_again = jnp.where(allowed[None], probs, 0.0)
        grad_values = jnp.einsum(
            "htu,thd->uhd", probs_again.astype(bf16), grad_mixed, preferred_element_type=f32
        )
        grad_probs = jnp.einsum("thd,uhd->htu", grad_mixed, values, preferred_element_type=f32)
        row_cross = jnp.sum(grad_probs * probs_again, axis=-1, keepdims=True)
        grad_scores = (probs_again * (grad_probs - row_cross)).astype(bf16)
        grad_queries = (
            jnp.einsum("htu,uhd->thd", grad_scores, keys_rot, preferred_element_type=f32) * scale
        )
        grad_keys = jnp.einsum("htu,thd->uhd", grad_scores, queries, preferred_element_type=f32) * scale
        grad_projected = jnp.stack(
            [
                rotate(grad_queries, cos_table, -sin_table, ROT),
                rotate(grad_keys, cos_table, -sin_table, ROT),
                grad_values,
            ],
            axis=1,
        )
        grad_projected = grad_projected.reshape(group_rows, 3, local_cols).astype(bf16)
        attend_bias_grad = jnp.sum(grad_projected.astype(f32), axis=0)
        attend_grad = jnp.einsum("td,tcn->dcn", branch_one, grad_projected, preferred_element_type=f32)
        grad_one = jnp.einsum("tcn,dcn->td", grad_projected, attend_full, preferred_element_type=f32)

        norm_partials = jnp.stack(
            [
                jnp.sum(grad_one * standard, axis=0),
                jnp.sum(grad_one, axis=0),
                jnp.sum(grad_two * standard, axis=0),
                jnp.sum(grad_two, axis=0),
            ]
        )
        norm_rows = (
            norm_partials.reshape(4, dp_count, tp_count, piece)
            .transpose(2, 0, 1, 3)
            .reshape(tp_count, 1, -1)
        )
        norm_len = norm_rows.shape[2]
        norm_rows = jnp.pad(norm_rows, ((0, 0), (0, 0), (0, 3 * width - norm_len)))
        token_parts = jnp.concatenate([partial_out, grad_one, grad_two], axis=1).reshape(
            tp_count, local_rows, 3 * width
        )
        reduced = lax.psum_scatter(
            jnp.concatenate([token_parts, norm_rows], axis=1).astype(bf16),
            "tensor",
            scatter_dimension=0,
        ).astype(f32)
        summed = reduced[:local_rows, :width]
        grad_one_local = reduced[:local_rows, width : 2 * width]
        grad_two_local = reduced[:local_rows, 2 * width :]
        norm_mine = reduced[local_rows, :norm_len].reshape(4, dp_count, piece).transpose(1, 0, 2)

        attend_bias_parts = (
            attend_bias_grad.reshape(3, dp_count, attend_bias.shape[1])
            .transpose(1, 0, 2)
            .reshape(dp_count, -1)
        )
        attn_grads = lax.psum_scatter(
            lane_rows(
                [
                    attend_grad.reshape(dp_count, -1),
                    output_grad.reshape(dp_count, -1),
                    attend_bias_parts,
                    norm_mine.reshape(dp_count, -1),
                ],
                axis=1,
            ).astype(bf16),
            "dp",
            scatter_dimension=0,
            tiled=True,
        ).reshape(-1).astype(f32)
        at = 0
        attend_weight_grad = attn_grads[at : at + attend_weight.size].reshape(attend_weight.shape)
        at += -(-attend_weight.size // 128) * 128
        output_weight_grad = attn_grads[at : at + output_weight.size].reshape(output_weight.shape)
        at += -(-output_weight.size // 128) * 128
        attend_bias_out = attn_grads[at : at + attend_bias.size].reshape(attend_bias.shape)
        at += -(-attend_bias.size // 128) * 128
        norm_grads = attn_grads[at : at + 4 * piece].reshape(4, piece)

        hidden_out = (hidden_in.astype(f32) + summed + out_bias_full + shrink_bias_full).astype(bf16)
        start = tensor_index * local_rows
        standard_local = lax.dynamic_slice_in_dim(standard, start, local_rows, 0)
        inverse_local = lax.dynamic_slice_in_dim(inverse_std, start, local_rows, 0)
        scaled = grad_one_local * gain_one + grad_two_local * gain_two
        input_grad = cotangent.astype(f32) + norm_backward(scaled, standard_local, inverse_local)
        return (
            hidden_out,
            input_grad,
            norm_grads[0],
            norm_grads[1],
            norm_grads[2],
            norm_grads[3],
            attend_weight_grad,
            attend_bias_out,
            output_weight_grad,
            out_bias_grad,
            expand_weight_grad,
            expand_bias_out,
            shrink_weight_grad,
            out_bias_grad,
        )
    in_specs = (
        P(("dp", "tensor"), None),
        P(("dp", "tensor"), None),
        P("dp", None),
        P("dp"),
        P(("dp", "tensor")),
        P(("dp", "tensor")),
        P(("dp", "tensor")),
        P(("dp", "tensor")),
        P("dp", None, "tensor"),
        P(None, ("tensor", "dp")),
        P("tensor", "dp"),
        P(("dp", "tensor")),
        P("dp", "tensor"),
        P(("tensor", "dp")),
        P("tensor", "dp"),
        P(("dp", "tensor")),
    )
    out_specs = (
        P(("dp", "tensor"), None),
        P(("dp", "tensor"), None),
        P(("dp", "tensor")),
        P(("dp", "tensor")),
        P(("dp", "tensor")),
        P(("dp", "tensor")),
        P("dp", None, "tensor"),
        P(None, ("tensor", "dp")),
        P("tensor", "dp"),
        P(("dp", "tensor")),
        P("dp", "tensor"),
        P(("tensor", "dp")),
        P("tensor", "dp"),
        P(("dp", "tensor")),
    )
    return jax.shard_map(
        per_device, mesh=mesh, in_specs=in_specs, out_specs=out_specs, check_vma=False
    )
```

```python
import jax
import jax.numpy as jnp
from jax import lax
from jax.sharding import PartitionSpec as P

HD = 64
ROT = 16


EPSILON = 1e-05
NEGATIVE = -1000000000.0


def rotate(tensor, cos_table, sin_table, rot_dims):
    half_dims = rot_dims // 2
    lower_half = tensor[..., :half_dims]
    upper_half = tensor[..., half_dims:rot_dims]
    return jnp.concatenate(
        [
            lower_half * cos_table - upper_half * sin_table,
            upper_half * cos_table + lower_half * sin_table,
            tensor[..., rot_dims:],
        ],
        axis=-1,
    )


def norm_backward(scaled, standard, inverse_std):
    mean_scaled = jnp.mean(scaled, axis=-1, keepdims=True)
    mean_cross = jnp.mean(scaled * standard, axis=-1, keepdims=True)
    return inverse_std * (scaled - mean_scaled - standard * mean_cross)


def lane_rows(parts, axis=1):
    padded = []
    for part in parts:
        extra = -part.shape[1] % 128
        padded.append(jnp.pad(part, ((0, 0), (0, extra))))
    joined = jnp.concatenate(padded, axis=axis)
    joined = joined.reshape(joined.shape[0], -1, 128)
    joined = jnp.pad(joined, ((0, 0), (0, -joined.shape[1] % 16), (0, 0)))
    return joined.reshape(-1, 128)


def gather_rows(parts, axis):
    flat, offsets, at = [], [], 0
    for part in parts:
        part = part.reshape(-1)
        extra = -part.shape[0] % 128
        flat.append(jnp.pad(part, (0, extra)))
        offsets.append(at)
        at += part.shape[0] + extra
    joined = jnp.concatenate(flat).reshape(-1, 128)
    joined = jnp.pad(joined, ((0, -joined.shape[0] % 16), (0, 0)))
    gathered = lax.all_gather(joined, axis, axis=0)
    return gathered.reshape(gathered.shape[0], -1), offsets


def solution(mesh):
    dp_count = mesh.shape["dp"]
    tp_count = mesh.shape["tensor"]

    def per_device(
        hidden_in,
        cotangent,
        segment_ids,
        live_count,
        first_gain,
        first_bias,
        second_gain,
        second_bias,
        attend_weight,
        attend_bias,
        output_weight,
        output_bias,
        expand_weight,
        expand_bias,
        shrink_weight,
        shrink_bias,
    ):
        f32 = jnp.float32
        bf16 = jnp.bfloat16
        local_rows, width = hidden_in.shape
        group_rows = local_rows * tp_count
        piece = first_gain.shape[0]
        dp_rows, _, local_cols = attend_weight.shape
        local_ff = expand_weight.shape[1]
        tensor_index = lax.axis_index("tensor")

        small = jnp.concatenate(
            [
                first_gain,
                first_bias,
                second_gain,
                second_bias,
                output_bias,
                shrink_bias,
                attend_bias.reshape(-1),
                expand_bias,
            ]
        )
        small_len = small.shape[0]
        small_row = jnp.zeros((1, width), bf16).at[0, :small_len].set(small)
        gathered = lax.all_gather(
            jnp.concatenate([hidden_in, cotangent, small_row], axis=0), "tensor", axis=0
        )
        rows_all = gathered[:, :local_rows].reshape(group_rows, width)
        grad_rows = gathered[:, local_rows : 2 * local_rows].reshape(group_rows, width)
        small_tensor = gathered[:, 2 * local_rows, :small_len]

        ffn_all, (expand_at, shrink_at, small_at) = gather_rows(
            [expand_weight, shrink_weight, small_tensor], "dp"
        )
        expand_full = ffn_all[:, expand_at : expand_at + expand_weight.size].reshape(
            dp_count * dp_rows, local_ff
        )
        shrink_parts = ffn_all[:, shrink_at : shrink_at + shrink_weight.size].reshape(
            dp_count, local_ff, dp_rows
        )
        small_all = ffn_all[:, small_at : small_at + small_tensor.size].reshape(
            dp_count, tp_count, small_len
        )

        def full_vector(k):
            return small_all[:, :, k * piece : (k + 1) * piece].reshape(-1).astype(f32)

        gain_one, bias_one, gain_two, bias_two, out_bias_full, shrink_bias_full = [
            full_vector(k) for k in range(6)
        ]
        small_mine = lax.dynamic_index_in_dim(small_all, tensor_index, axis=1, keepdims=False)
        attend_bias_full = (
            small_mine[:, 6 * piece : 6 * piece + attend_bias.size]
            .reshape(dp_count, 3, attend_bias.shape[1])
            .transpose(1, 0, 2)
            .reshape(3, local_cols)
        )
        expand_bias_full = small_mine[:, 6 * piece + attend_bias.size :].reshape(-1)

        attend_all, (attend_at, output_at) = gather_rows([attend_weight, output_weight], "dp")
        attend_full = attend_all[:, attend_at : attend_at + attend_weight.size].reshape(
            dp_count * dp_rows, 3, local_cols
        )
        output_parts = attend_all[:, output_at : output_at + output_weight.size].reshape(
            dp_count, local_cols, dp_rows
        )

        local_heads = local_cols // HD
        scale = HD ** (-0.5)
        rows_float = rows_all.astype(f32)
        centre = rows_float - jnp.mean(rows_float, axis=-1, keepdims=True)
        inverse_std = lax.rsqrt(jnp.mean(centre * centre, axis=-1, keepdims=True) + EPSILON)
        standard = centre * inverse_std
        branch_one = (standard * gain_one + bias_one).astype(bf16)
        branch_two = (standard * gain_two + bias_two).astype(bf16)
        grad_rows_parts = grad_rows.reshape(group_rows, dp_count, dp_rows)

        expanded = jnp.dot(
            branch_two, expand_full, preferred_element_type=f32
        ) + expand_bias_full.astype(f32)
        activated, gelu_back = jax.vjp(lambda value: jax.nn.gelu(value, approximate=False), expanded)
        activated_low = activated.astype(bf16)
        ffn_out = jnp.einsum(
            "tf,kfe->tke", activated_low, shrink_parts, preferred_element_type=f32
        ).reshape(group_rows, width)
        grad_activated = jnp.einsum(
            "tke,kfe->tf", grad_rows_parts, shrink_parts, preferred_element_type=f32
        )
        shrink_grad = jnp.einsum(
            "tf,tke->kfe", activated_low, grad_rows_parts, preferred_element_type=f32
        )
        grad_expanded = gelu_back(grad_activated)[0].astype(bf16)
        expand_bias_grad = jnp.sum(grad_expanded.astype(f32), axis=0)
        expand_grad = jnp.einsum("td,tf->df", branch_two, grad_expanded, preferred_element_type=f32)
        grad_two = jnp.einsum("tf,df->td", grad_expanded, expand_full, preferred_element_type=f32)
        out_bias_sum = jnp.sum(grad_rows.astype(f32), axis=0).reshape(dp_count, tp_count, piece)
        out_bias_mine = lax.dynamic_index_in_dim(out_bias_sum, tensor_index, axis=1, keepdims=False)
        ffn_grads = lax.psum_scatter(
            lane_rows(
                [
                    expand_grad.reshape(dp_count, -1),
                    shrink_grad.reshape(dp_count, -1),
                    expand_bias_grad.reshape(dp_count, -1),
                    out_bias_mine,
                ],
                axis=1,
            ).astype(bf16),
            "dp",
            scatter_dimension=0,
            tiled=True,
        ).reshape(-1).astype(f32)
        at = 0
        expand_weight_grad = ffn_grads[at : at + expand_weight.size].reshape(expand_weight.shape)
        at += -(-expand_weight.size // 128) * 128
        shrink_weight_grad = ffn_grads[at : at + shrink_weight.size].reshape(shrink_weight.shape)
        at += -(-shrink_weight.size // 128) * 128
        expand_bias_out = ffn_grads[at : at + expand_bias.size]
        at += -(-expand_bias.size // 128) * 128
        out_bias_grad = ffn_grads[at : at + piece]

        projected = (
            jnp.einsum("td,dcn->tcn", branch_one, attend_full, preferred_element_type=f32)
            + attend_bias_full.astype(f32)[None]
        )
        segments = segment_ids[0]
        index = jnp.arange(group_rows)
        same_seq = segments[:, None] == segments[None, :]
        positions = jnp.sum((same_seq & (index[None, :] < index[:, None])).astype(f32), axis=1)
        allowed = (
            same_seq
            & (index[None, :] <= index[:, None])
            & ((index[None, :] < live_count[0]) | (index[None, :] == index[:, None]))
        )
        half_dims = ROT // 2
        inverse = 10000.0 ** (-jnp.arange(half_dims).astype(f32) * 2.0 / ROT)
        angles = positions[:, None] * inverse[None, :]
        cos_table = jnp.cos(angles)[:, None, :]
        sin_table = jnp.sin(angles)[:, None, :]
        per_head = projected.reshape(group_rows, 3, local_heads, HD)
        queries = rotate(per_head[:, 0], cos_table, sin_table, ROT).astype(bf16)
        keys_rot = rotate(per_head[:, 1], cos_table, sin_table, ROT).astype(bf16)
        values = per_head[:, 2].astype(bf16)
        scores = jnp.einsum("thd,uhd->htu", queries, keys_rot, preferred_element_type=f32) * scale
        scores = jnp.where(allowed[None], scores, NEGATIVE)
        top_score = jnp.max(scores, axis=-1, keepdims=True)
        log_total = top_score + jnp.log(jnp.sum(jnp.exp(scores - top_score), axis=-1, keepdims=True))
        probs = jnp.exp(scores - log_total)
        mixed = jnp.einsum("htu,uhd->thd", probs.astype(bf16), values, preferred_element_type=f32)
        mixed = mixed.reshape(group_rows, local_heads * HD).astype(bf16)
        partial_out = ffn_out + jnp.einsum(
            "tn,kne->tke", mixed, output_parts, preferred_element_type=f32
        ).reshape(group_rows, width)
        summed = lax.psum_scatter(
            partial_out.astype(bf16), "tensor", scatter_dimension=0, tiled=True
        ).astype(f32)

        grad_mixed = jnp.einsum(
            "tke,kne->tn", grad_rows_parts, output_parts, preferred_element_type=f32
        ).astype(bf16)
        output_grad = jnp.einsum("tn,tke->kne", mixed, grad_rows_parts, preferred_element_type=f32)
        grad_mixed = grad_mixed.reshape(group_rows, local_heads, HD)
        probs_again = jnp.where(allowed[None], probs, 0.0)
        grad_values = jnp.einsum(
            "htu,thd->uhd", probs_again.astype(bf16), grad_mixed, preferred_element_type=f32
        )
        grad_probs = jnp.einsum("thd,uhd->htu", grad_mixed, values, preferred_element_type=f32)
        row_cross = jnp.sum(grad_probs * probs_again, axis=-1, keepdims=True)
        grad_scores = (probs_again * (grad_probs - row_cross)).astype(bf16)
        grad_queries = (
            jnp.einsum("htu,uhd->thd", grad_scores, keys_rot, preferred_element_type=f32) * scale
        )
        grad_keys = jnp.einsum("htu,thd->uhd", grad_scores, queries, preferred_element_type=f32) * scale
        grad_projected = jnp.stack(
            [
                rotate(grad_queries, cos_table, -sin_table, ROT),
                rotate(grad_keys, cos_table, -sin_table, ROT),
                grad_values,
            ],
            axis=1,
        )
        grad_projected = grad_projected.reshape(group_rows, 3, local_cols).astype(bf16)
        attend_bias_grad = jnp.sum(grad_projected.astype(f32), axis=0)
        attend_grad = jnp.einsum("td,tcn->dcn", branch_one, grad_projected, preferred_element_type=f32)
        grad_one = jnp.einsum("tcn,dcn->td", grad_projected, attend_full, preferred_element_type=f32)

        norm_partials = jnp.stack(
            [
                jnp.sum(grad_one * standard, axis=0),
                jnp.sum(grad_one, axis=0),
                jnp.sum(grad_two * standard, axis=0),
                jnp.sum(grad_two, axis=0),
            ]
        )
        norm_rows = (
            norm_partials.reshape(4, dp_count, tp_count, piece)
            .transpose(2, 0, 1, 3)
            .reshape(tp_count, 1, -1)
        )
        norm_len = norm_rows.shape[2]
        norm_rows = jnp.pad(norm_rows, ((0, 0), (0, 0), (0, width - norm_len)))
        scaled_parts = (grad_one * gain_one + grad_two * gain_two).reshape(
            tp_count, local_rows, width
        )
        reduced = lax.psum_scatter(
            jnp.concatenate([scaled_parts, norm_rows], axis=1).astype(bf16),
            "tensor",
            scatter_dimension=0,
        ).astype(f32)
        scaled = reduced[:local_rows]
        norm_mine = reduced[local_rows, :norm_len].reshape(4, dp_count, piece).transpose(1, 0, 2)

        attend_bias_parts = (
            attend_bias_grad.reshape(3, dp_count, attend_bias.shape[1])
            .transpose(1, 0, 2)
            .reshape(dp_count, -1)
        )
        attn_grads = lax.psum_scatter(
            lane_rows(
                [
                    attend_grad.reshape(dp_count, -1),
                    output_grad.reshape(dp_count, -1),
                    attend_bias_parts,
                    norm_mine.reshape(dp_count, -1),
                ],
                axis=1,
            ).astype(bf16),
            "dp",
            scatter_dimension=0,
            tiled=True,
        ).reshape(-1).astype(f32)
        at = 0
        attend_weight_grad = attn_grads[at : at + attend_weight.size].reshape(attend_weight.shape)
        at += -(-attend_weight.size // 128) * 128
        output_weight_grad = attn_grads[at : at + output_weight.size].reshape(output_weight.shape)
        at += -(-output_weight.size // 128) * 128
        attend_bias_out = attn_grads[at : at + attend_bias.size].reshape(attend_bias.shape)
        at += -(-attend_bias.size // 128) * 128
        norm_grads = attn_grads[at : at + 4 * piece].reshape(4, piece)

        hidden_out = (hidden_in.astype(f32) + summed + out_bias_full + shrink_bias_full).astype(bf16)
        start = tensor_index * local_rows
        standard_local = lax.dynamic_slice_in_dim(standard, start, local_rows, 0)
        inverse_local = lax.dynamic_slice_in_dim(inverse_std, start, local_rows, 0)
        input_grad = cotangent.astype(f32) + norm_backward(scaled, standard_local, inverse_local)
        return (
            hidden_out,
            input_grad,
            norm_grads[0],
            norm_grads[1],
            norm_grads[2],
            norm_grads[3],
            attend_weight_grad,
            attend_bias_out,
            output_weight_grad,
            out_bias_grad,
            expand_weight_grad,
            expand_bias_out,
            shrink_weight_grad,
            out_bias_grad,
        )
    in_specs = (
        P(("dp", "tensor"), None),
        P(("dp", "tensor"), None),
        P("dp", None),
        P("dp"),
        P(("dp", "tensor")),
        P(("dp", "tensor")),
        P(("dp", "tensor")),
        P(("dp", "tensor")),
        P("dp", None, "tensor"),
        P(None, ("tensor", "dp")),
        P("tensor", "dp"),
        P(("dp", "tensor")),
        P("dp", "tensor"),
        P(("tensor", "dp")),
        P("tensor", "dp"),
        P(("dp", "tensor")),
    )
    out_specs = (
        P(("dp", "tensor"), None),
        P(("dp", "tensor"), None),
        P(("dp", "tensor")),
        P(("dp", "tensor")),
        P(("dp", "tensor")),
        P(("dp", "tensor")),
        P("dp", None, "tensor"),
        P(None, ("tensor", "dp")),
        P("tensor", "dp"),
        P(("dp", "tensor")),
        P("dp", "tensor"),
        P(("tensor", "dp")),
        P("tensor", "dp"),
        P(("dp", "tensor")),
    )
    return jax.shard_map(
        per_device, mesh=mesh, in_specs=in_specs, out_specs=out_specs, check_vma=False
    )
```

```python
import jax
import jax.numpy as jnp
from jax import lax
from jax.sharding import PartitionSpec as P

HD = 64
ROT = 16


EPSILON = 1e-05
NEGATIVE = -1000000000.0


def rotate(tensor, cos_table, sin_table, rot_dims):
    half_dims = rot_dims // 2
    lower_half = tensor[..., :half_dims]
    upper_half = tensor[..., half_dims:rot_dims]
    return jnp.concatenate(
        [
            lower_half * cos_table - upper_half * sin_table,
            upper_half * cos_table + lower_half * sin_table,
            tensor[..., rot_dims:],
        ],
        axis=-1,
    )


def norm_backward(scaled, standard, inverse_std):
    mean_scaled = jnp.mean(scaled, axis=-1, keepdims=True)
    mean_cross = jnp.mean(scaled * standard, axis=-1, keepdims=True)
    return inverse_std * (scaled - mean_scaled - standard * mean_cross)


def lane_rows(parts, axis=1):
    padded = []
    for part in parts:
        extra = -part.shape[1] % 128
        padded.append(jnp.pad(part, ((0, 0), (0, extra))))
    joined = jnp.concatenate(padded, axis=axis)
    joined = joined.reshape(joined.shape[0], -1, 128)
    joined = jnp.pad(joined, ((0, 0), (0, -joined.shape[1] % 16), (0, 0)))
    return joined.reshape(-1, 128)


def gather_rows(parts, axis):
    flat, offsets, at = [], [], 0
    for part in parts:
        part = part.reshape(-1)
        extra = -part.shape[0] % 128
        flat.append(jnp.pad(part, (0, extra)))
        offsets.append(at)
        at += part.shape[0] + extra
    joined = jnp.concatenate(flat).reshape(-1, 128)
    joined = jnp.pad(joined, ((0, -joined.shape[0] % 16), (0, 0)))
    gathered = lax.all_gather(joined, axis, axis=0)
    return gathered.reshape(gathered.shape[0], -1), offsets


def solution(mesh):
    dp_count = mesh.shape["dp"]
    tp_count = mesh.shape["tensor"]

    def per_device(
        hidden_in,
        cotangent,
        segment_ids,
        live_count,
        first_gain,
        first_bias,
        second_gain,
        second_bias,
        attend_weight,
        attend_bias,
        output_weight,
        output_bias,
        expand_weight,
        expand_bias,
        shrink_weight,
        shrink_bias,
    ):
        f32 = jnp.float32
        bf16 = jnp.bfloat16
        local_rows, width = hidden_in.shape
        group_rows = local_rows * tp_count
        piece = first_gain.shape[0]
        dp_rows, _, local_cols = attend_weight.shape
        local_ff = expand_weight.shape[1]
        tensor_index = lax.axis_index("tensor")

        small = jnp.concatenate(
            [
                first_gain,
                first_bias,
                second_gain,
                second_bias,
                output_bias,
                shrink_bias,
                attend_bias.reshape(-1),
                expand_bias,
            ]
        )
        small_len = small.shape[0]
        small_row = jnp.zeros((1, width), bf16).at[0, :small_len].set(small)
        gathered = lax.all_gather(
            jnp.concatenate([hidden_in, cotangent, small_row], axis=0), "tensor", axis=0
        )
        rows_all = gathered[:, :local_rows].reshape(group_rows, width)
        grad_rows = gathered[:, local_rows : 2 * local_rows].reshape(group_rows, width)
        small_tensor = gathered[:, 2 * local_rows, :small_len]

        attend_all, (attend_at, output_at, small_at) = gather_rows(
            [attend_weight, output_weight, small_tensor], "dp"
        )
        attend_full = attend_all[:, attend_at : attend_at + attend_weight.size].reshape(
            dp_count * dp_rows, 3, local_cols
        )
        output_parts = attend_all[:, output_at : output_at + output_weight.size].reshape(
            dp_count, local_cols, dp_rows
        )
        small_all = attend_all[:, small_at : small_at + small_tensor.size].reshape(
            dp_count, tp_count, small_len
        )

        def full_vector(k):
            return small_all[:, :, k * piece : (k + 1) * piece].reshape(-1).astype(f32)

        gain_one, bias_one, gain_two, bias_two, out_bias_full, shrink_bias_full = [
            full_vector(k) for k in range(6)
        ]
        small_mine = lax.dynamic_index_in_dim(small_all, tensor_index, axis=1, keepdims=False)
        attend_bias_full = (
            small_mine[:, 6 * piece : 6 * piece + attend_bias.size]
            .reshape(dp_count, 3, attend_bias.shape[1])
            .transpose(1, 0, 2)
            .reshape(3, local_cols)
        )
        expand_bias_full = small_mine[:, 6 * piece + attend_bias.size :].reshape(-1)

        ffn_all, (expand_at, shrink_at) = gather_rows([expand_weight, shrink_weight], "dp")
        expand_full = ffn_all[:, expand_at : expand_at + expand_weight.size].reshape(
            dp_count * dp_rows, local_ff
        )
        shrink_parts = ffn_all[:, shrink_at : shrink_at + shrink_weight.size].reshape(
            dp_count, local_ff, dp_rows
        )

        local_heads = local_cols // HD
        scale = HD ** (-0.5)
        rows_float = rows_all.astype(f32)
        centre = rows_float - jnp.mean(rows_float, axis=-1, keepdims=True)
        inverse_std = lax.rsqrt(jnp.mean(centre * centre, axis=-1, keepdims=True) + EPSILON)
        standard = centre * inverse_std
        branch_one = (standard * gain_one + bias_one).astype(bf16)
        branch_two = (standard * gain_two + bias_two).astype(bf16)
        grad_rows_parts = grad_rows.reshape(group_rows, dp_count, dp_rows)

        projected = (
            jnp.einsum("td,dcn->tcn", branch_one, attend_full, preferred_element_type=f32)
            + attend_bias_full.astype(f32)[None]
        )
        segments = segment_ids[0]
        index = jnp.arange(group_rows)
        same_seq = segments[:, None] == segments[None, :]
        positions = jnp.sum((same_seq & (index[None, :] < index[:, None])).astype(f32), axis=1)
        allowed = (
            same_seq
            & (index[None, :] <= index[:, None])
            & ((index[None, :] < live_count[0]) | (index[None, :] == index[:, None]))
        )
        half_dims = ROT // 2
        inverse = 10000.0 ** (-jnp.arange(half_dims).astype(f32) * 2.0 / ROT)
        angles = positions[:, None] * inverse[None, :]
        cos_table = jnp.cos(angles)[:, None, :]
        sin_table = jnp.sin(angles)[:, None, :]
        per_head = projected.reshape(group_rows, 3, local_heads, HD)
        queries = rotate(per_head[:, 0], cos_table, sin_table, ROT).astype(bf16)
        keys_rot = rotate(per_head[:, 1], cos_table, sin_table, ROT).astype(bf16)
        values = per_head[:, 2].astype(bf16)
        scores = jnp.einsum("thd,uhd->htu", queries, keys_rot, preferred_element_type=f32) * scale
        scores = jnp.where(allowed[None], scores, NEGATIVE)
        top_score = jnp.max(scores, axis=-1, keepdims=True)
        log_total = top_score + jnp.log(jnp.sum(jnp.exp(scores - top_score), axis=-1, keepdims=True))
        probs = jnp.exp(scores - log_total)
        mixed = jnp.einsum("htu,uhd->thd", probs.astype(bf16), values, preferred_element_type=f32)
        mixed = mixed.reshape(group_rows, local_heads * HD).astype(bf16)
        attn_out = jnp.einsum(
            "tn,kne->tke", mixed, output_parts, preferred_element_type=f32
        ).reshape(group_rows, width)

        grad_mixed = jnp.einsum(
            "tke,kne->tn", grad_rows_parts, output_parts, preferred_element_type=f32
        ).astype(bf16)
        output_grad = jnp.einsum("tn,tke->kne", mixed, grad_rows_parts, preferred_element_type=f32)
        grad_mixed = grad_mixed.reshape(group_rows, local_heads, HD)
        probs_again = jnp.where(allowed[None], probs, 0.0)
        grad_values = jnp.einsum(
            "htu,thd->uhd", probs_again.astype(bf16), grad_mixed, preferred_element_type=f32
        )
        grad_probs = jnp.einsum("thd,uhd->htu", grad_mixed, values, preferred_element_type=f32)
        row_cross = jnp.sum(grad_probs * probs_again, axis=-1, keepdims=True)
        grad_scores = (probs_again * (grad_probs - row_cross)).astype(bf16)
        grad_queries = (
            jnp.einsum("htu,uhd->thd", grad_scores, keys_rot, preferred_element_type=f32) * scale
        )
        grad_keys = jnp.einsum("htu,thd->uhd", grad_scores, queries, preferred_element_type=f32) * scale
        grad_projected = jnp.stack(
            [
                rotate(grad_queries, cos_table, -sin_table, ROT),
                rotate(grad_keys, cos_table, -sin_table, ROT),
                grad_values,
            ],
            axis=1,
        )
        grad_projected = grad_projected.reshape(group_rows, 3, local_cols).astype(bf16)
        attend_bias_grad = jnp.sum(grad_projected.astype(f32), axis=0)
        attend_grad = jnp.einsum("td,tcn->dcn", branch_one, grad_projected, preferred_element_type=f32)
        grad_one = jnp.einsum("tcn,dcn->td", grad_projected, attend_full, preferred_element_type=f32)

        attend_bias_parts = (
            attend_bias_grad.reshape(3, dp_count, attend_bias.shape[1])
            .transpose(1, 0, 2)
            .reshape(dp_count, -1)
        )
        attn_payload = lane_rows(
            [attend_grad.reshape(dp_count, -1), output_grad.reshape(dp_count, -1), attend_bias_parts],
            axis=1,
        ).astype(bf16)
        expand_full, shrink_parts, _ = lax.optimization_barrier(
            (expand_full, shrink_parts, attn_payload)
        )

        expanded = jnp.dot(
            branch_two, expand_full, preferred_element_type=f32
        ) + expand_bias_full.astype(f32)
        activated, gelu_back = jax.vjp(lambda value: jax.nn.gelu(value, approximate=False), expanded)
        activated_low = activated.astype(bf16)
        ffn_out = jnp.einsum(
            "tf,kfe->tke", activated_low, shrink_parts, preferred_element_type=f32
        ).reshape(group_rows, width)
        grad_activated = jnp.einsum(
            "tke,kfe->tf", grad_rows_parts, shrink_parts, preferred_element_type=f32
        )
        shrink_grad = jnp.einsum(
            "tf,tke->kfe", activated_low, grad_rows_parts, preferred_element_type=f32
        )
        grad_expanded = gelu_back(grad_activated)[0].astype(bf16)
        expand_bias_grad = jnp.sum(grad_expanded.astype(f32), axis=0)
        expand_grad = jnp.einsum("td,tf->df", branch_two, grad_expanded, preferred_element_type=f32)
        grad_two = jnp.einsum("tf,df->td", grad_expanded, expand_full, preferred_element_type=f32)
        out_bias_sum = jnp.sum(grad_rows.astype(f32), axis=0).reshape(dp_count, tp_count, piece)
        out_bias_mine = lax.dynamic_index_in_dim(out_bias_sum, tensor_index, axis=1, keepdims=False)

        partial_out = ffn_out + attn_out

        norm_partials = jnp.stack(
            [
                jnp.sum(grad_one * standard, axis=0),
                jnp.sum(grad_one, axis=0),
                jnp.sum(grad_two * standard, axis=0),
                jnp.sum(grad_two, axis=0),
            ]
        )
        norm_rows = (
            norm_partials.reshape(4, dp_count, tp_count, piece)
            .transpose(2, 0, 1, 3)
            .reshape(tp_count, 1, -1)
        )
        norm_len = norm_rows.shape[2]
        norm_rows = jnp.pad(norm_rows, ((0, 0), (0, 0), (0, 2 * width - norm_len)))
        scaled_parts = grad_one * gain_one + grad_two * gain_two
        token_parts = jnp.concatenate([partial_out, scaled_parts], axis=1).reshape(
            tp_count, local_rows, 2 * width
        )
        attn_reduced = lax.psum_scatter(attn_payload, "dp", scatter_dimension=0, tiled=True)
        attn_reduced, token_parts = lax.optimization_barrier((attn_reduced, token_parts))
        attn_grads = attn_reduced.reshape(-1).astype(f32)
        reduced = lax.psum_scatter(
            jnp.concatenate([token_parts, norm_rows], axis=1).astype(bf16),
            "tensor",
            scatter_dimension=0,
        ).astype(f32)
        summed = reduced[:local_rows, :width]
        scaled = reduced[:local_rows, width:]
        norm_mine = reduced[local_rows, :norm_len].reshape(4, dp_count, piece).transpose(1, 0, 2)

        at = 0
        attend_weight_grad = attn_grads[at : at + attend_weight.size].reshape(attend_weight.shape)
        at += -(-attend_weight.size // 128) * 128
        output_weight_grad = attn_grads[at : at + output_weight.size].reshape(output_weight.shape)
        at += -(-output_weight.size // 128) * 128
        attend_bias_out = attn_grads[at : at + attend_bias.size].reshape(attend_bias.shape)


        ffn_grads = lax.psum_scatter(
            lane_rows(
                [
                    expand_grad.reshape(dp_count, -1),
                    shrink_grad.reshape(dp_count, -1),
                    expand_bias_grad.reshape(dp_count, -1),
                    out_bias_mine,
                    norm_mine.reshape(dp_count, -1),
                ],
                axis=1,
            ).astype(bf16),
            "dp",
            scatter_dimension=0,
            tiled=True,
        ).reshape(-1).astype(f32)
        at = 0
        expand_weight_grad = ffn_grads[at : at + expand_weight.size].reshape(expand_weight.shape)
        at += -(-expand_weight.size // 128) * 128
        shrink_weight_grad = ffn_grads[at : at + shrink_weight.size].reshape(shrink_weight.shape)
        at += -(-shrink_weight.size // 128) * 128
        expand_bias_out = ffn_grads[at : at + expand_bias.size]
        at += -(-expand_bias.size // 128) * 128
        out_bias_grad = ffn_grads[at : at + piece]
        at += -(-piece // 128) * 128
        norm_grads = ffn_grads[at : at + 4 * piece].reshape(4, piece)

        hidden_out = (hidden_in.astype(f32) + summed + out_bias_full + shrink_bias_full).astype(bf16)
        start = tensor_index * local_rows
        standard_local = lax.dynamic_slice_in_dim(standard, start, local_rows, 0)
        inverse_local = lax.dynamic_slice_in_dim(inverse_std, start, local_rows, 0)
        input_grad = cotangent.astype(f32) + norm_backward(scaled, standard_local, inverse_local)
        return (
            hidden_out,
            input_grad,
            norm_grads[0],
            norm_grads[1],
            norm_grads[2],
            norm_grads[3],
            attend_weight_grad,
            attend_bias_out,
            output_weight_grad,
            out_bias_grad,
            expand_weight_grad,
            expand_bias_out,
            shrink_weight_grad,
            out_bias_grad,
        )
    in_specs = (
        P(("dp", "tensor"), None),
        P(("dp", "tensor"), None),
        P("dp", None),
        P("dp"),
        P(("dp", "tensor")),
        P(("dp", "tensor")),
        P(("dp", "tensor")),
        P(("dp", "tensor")),
        P("dp", None, "tensor"),
        P(None, ("tensor", "dp")),
        P("tensor", "dp"),
        P(("dp", "tensor")),
        P("dp", "tensor"),
        P(("tensor", "dp")),
        P("tensor", "dp"),
        P(("dp", "tensor")),
    )
    out_specs = (
        P(("dp", "tensor"), None),
        P(("dp", "tensor"), None),
        P(("dp", "tensor")),
        P(("dp", "tensor")),
        P(("dp", "tensor")),
        P(("dp", "tensor")),
        P("dp", None, "tensor"),
        P(None, ("tensor", "dp")),
        P("tensor", "dp"),
        P(("dp", "tensor")),
        P("dp", "tensor"),
        P(("tensor", "dp")),
        P("tensor", "dp"),
        P(("dp", "tensor")),
    )
    return jax.shard_map(
        per_device, mesh=mesh, in_specs=in_specs, out_specs=out_specs, check_vma=False
    )
```

```python
import jax
import jax.numpy as jnp
from jax import lax
from jax.sharding import PartitionSpec as P

HD = 64
ROT = 16


EPSILON = 1e-05
NEGATIVE = -1000000000.0


def rotate(tensor, cos_table, sin_table, rot_dims):
    half_dims = rot_dims // 2
    lower_half = tensor[..., :half_dims]
    upper_half = tensor[..., half_dims:rot_dims]
    return jnp.concatenate(
        [
            lower_half * cos_table - upper_half * sin_table,
            upper_half * cos_table + lower_half * sin_table,
            tensor[..., rot_dims:],
        ],
        axis=-1,
    )


def norm_backward(scaled, standard, inverse_std):
    mean_scaled = jnp.mean(scaled, axis=-1, keepdims=True)
    mean_cross = jnp.mean(scaled * standard, axis=-1, keepdims=True)
    return inverse_std * (scaled - mean_scaled - standard * mean_cross)


def lane_rows(parts, axis=1):
    padded = []
    for part in parts:
        extra = -part.shape[1] % 128
        padded.append(jnp.pad(part, ((0, 0), (0, extra))))
    joined = jnp.concatenate(padded, axis=axis)
    joined = joined.reshape(joined.shape[0], -1, 128)
    joined = jnp.pad(joined, ((0, 0), (0, -joined.shape[1] % 16), (0, 0)))
    return joined.reshape(-1, 128)


def gather_rows(parts, axis):
    flat, offsets, at = [], [], 0
    for part in parts:
        part = part.reshape(-1)
        extra = -part.shape[0] % 128
        flat.append(jnp.pad(part, (0, extra)))
        offsets.append(at)
        at += part.shape[0] + extra
    joined = jnp.concatenate(flat).reshape(-1, 128)
    joined = jnp.pad(joined, ((0, -joined.shape[0] % 16), (0, 0)))
    gathered = lax.all_gather(joined, axis, axis=0)
    return gathered.reshape(gathered.shape[0], -1), offsets


def ring_gather(block, axis, count, index):
    parts = [block] + [
        lax.ppermute(block, axis, [(j, (j + k) % count) for j in range(count)])
        for k in range(1, count)
    ]
    backward = jnp.stack([parts[0]] + parts[:0:-1])
    doubled = jnp.concatenate([backward, backward])
    return lax.dynamic_slice_in_dim(doubled, (count - index) % count, count, 0)


def ring_reduce(chunks, axis, count, index):
    total = lax.dynamic_index_in_dim(chunks, index, 0, keepdims=False).astype(jnp.float32)
    for k in range(1, count):
        send = lax.dynamic_index_in_dim(chunks, (index + k) % count, 0, keepdims=False)
        moved = lax.ppermute(send, axis, [(j, (j + k) % count) for j in range(count)])
        total = total + moved.astype(jnp.float32)
    return total


def solution(mesh):
    dp_count = mesh.shape["dp"]
    tp_count = mesh.shape["tensor"]

    def per_device(
        hidden_in,
        cotangent,
        segment_ids,
        live_count,
        first_gain,
        first_bias,
        second_gain,
        second_bias,
        attend_weight,
        attend_bias,
        output_weight,
        output_bias,
        expand_weight,
        expand_bias,
        shrink_weight,
        shrink_bias,
    ):
        f32 = jnp.float32
        bf16 = jnp.bfloat16
        local_rows, width = hidden_in.shape
        group_rows = local_rows * tp_count
        piece = first_gain.shape[0]
        dp_rows, _, local_cols = attend_weight.shape
        local_ff = expand_weight.shape[1]
        tensor_index = lax.axis_index("tensor")

        small = jnp.concatenate(
            [
                first_gain,
                first_bias,
                second_gain,
                second_bias,
                output_bias,
                shrink_bias,
                attend_bias.reshape(-1),
                expand_bias,
            ]
        )
        small_len = small.shape[0]
        gathered = ring_gather(
            jnp.concatenate([hidden_in, cotangent], axis=0), "tensor", tp_count, tensor_index
        )
        rows_all = gathered[:, :local_rows].reshape(group_rows, width)
        grad_rows = gathered[:, local_rows:].reshape(group_rows, width)

        attend_all, (attend_at, output_at, small_at) = gather_rows(
            [attend_weight, output_weight, small], "dp"
        )
        attend_full = attend_all[:, attend_at : attend_at + attend_weight.size].reshape(
            dp_count * dp_rows, 3, local_cols
        )
        output_parts = attend_all[:, output_at : output_at + output_weight.size].reshape(
            dp_count, local_cols, dp_rows
        )
        small_all = ring_gather(
            attend_all[:, small_at : small_at + small_len], "tensor", tp_count, tensor_index
        ).transpose(1, 0, 2)

        def full_vector(k):
            return small_all[:, :, k * piece : (k + 1) * piece].reshape(-1).astype(f32)

        gain_one, bias_one, gain_two, bias_two, out_bias_full, shrink_bias_full = [
            full_vector(k) for k in range(6)
        ]
        small_mine = lax.dynamic_index_in_dim(small_all, tensor_index, axis=1, keepdims=False)
        attend_bias_full = (
            small_mine[:, 6 * piece : 6 * piece + attend_bias.size]
            .reshape(dp_count, 3, attend_bias.shape[1])
            .transpose(1, 0, 2)
            .reshape(3, local_cols)
        )
        expand_bias_full = small_mine[:, 6 * piece + attend_bias.size :].reshape(-1)

        ffn_all, (expand_at, shrink_at) = gather_rows([expand_weight, shrink_weight], "dp")
        expand_full = ffn_all[:, expand_at : expand_at + expand_weight.size].reshape(
            dp_count * dp_rows, local_ff
        )
        shrink_parts = ffn_all[:, shrink_at : shrink_at + shrink_weight.size].reshape(
            dp_count, local_ff, dp_rows
        )

        local_heads = local_cols // HD
        scale = HD ** (-0.5)
        rows_float = rows_all.astype(f32)
        centre = rows_float - jnp.mean(rows_float, axis=-1, keepdims=True)
        inverse_std = lax.rsqrt(jnp.mean(centre * centre, axis=-1, keepdims=True) + EPSILON)
        standard = centre * inverse_std
        branch_one = (standard * gain_one + bias_one).astype(bf16)
        branch_two = (standard * gain_two + bias_two).astype(bf16)
        grad_rows_parts = grad_rows.reshape(group_rows, dp_count, dp_rows)

        projected = (
            jnp.einsum("td,dcn->tcn", branch_one, attend_full, preferred_element_type=f32)
            + attend_bias_full.astype(f32)[None]
        )
        segments = segment_ids[0]
        index = jnp.arange(group_rows)
        same_seq = segments[:, None] == segments[None, :]
        positions = jnp.sum((same_seq & (index[None, :] < index[:, None])).astype(f32), axis=1)
        allowed = (
            same_seq
            & (index[None, :] <= index[:, None])
            & ((index[None, :] < live_count[0]) | (index[None, :] == index[:, None]))
        )
        half_dims = ROT // 2
        inverse = 10000.0 ** (-jnp.arange(half_dims).astype(f32) * 2.0 / ROT)
        angles = positions[:, None] * inverse[None, :]
        cos_table = jnp.cos(angles)[:, None, :]
        sin_table = jnp.sin(angles)[:, None, :]
        per_head = projected.reshape(group_rows, 3, local_heads, HD)
        queries = rotate(per_head[:, 0], cos_table, sin_table, ROT).astype(bf16)
        keys_rot = rotate(per_head[:, 1], cos_table, sin_table, ROT).astype(bf16)
        values = per_head[:, 2].astype(bf16)
        scores = jnp.einsum("thd,uhd->htu", queries, keys_rot, preferred_element_type=f32) * scale
        scores = jnp.where(allowed[None], scores, NEGATIVE)
        top_score = jnp.max(scores, axis=-1, keepdims=True)
        log_total = top_score + jnp.log(jnp.sum(jnp.exp(scores - top_score), axis=-1, keepdims=True))
        probs = jnp.exp(scores - log_total)
        mixed = jnp.einsum("htu,uhd->thd", probs.astype(bf16), values, preferred_element_type=f32)
        mixed = mixed.reshape(group_rows, local_heads * HD).astype(bf16)
        attn_out = jnp.einsum(
            "tn,kne->tke", mixed, output_parts, preferred_element_type=f32
        ).reshape(group_rows, width)

        grad_mixed = jnp.einsum(
            "tke,kne->tn", grad_rows_parts, output_parts, preferred_element_type=f32
        ).astype(bf16)
        output_grad = jnp.einsum("tn,tke->kne", mixed, grad_rows_parts, preferred_element_type=f32)
        grad_mixed = grad_mixed.reshape(group_rows, local_heads, HD)
        probs_again = jnp.where(allowed[None], probs, 0.0)
        grad_values = jnp.einsum(
            "htu,thd->uhd", probs_again.astype(bf16), grad_mixed, preferred_element_type=f32
        )
        grad_probs = jnp.einsum("thd,uhd->htu", grad_mixed, values, preferred_element_type=f32)
        row_cross = jnp.sum(grad_probs * probs_again, axis=-1, keepdims=True)
        grad_scores = (probs_again * (grad_probs - row_cross)).astype(bf16)
        grad_queries = (
            jnp.einsum("htu,uhd->thd", grad_scores, keys_rot, preferred_element_type=f32) * scale
        )
        grad_keys = jnp.einsum("htu,thd->uhd", grad_scores, queries, preferred_element_type=f32) * scale
        grad_projected = jnp.stack(
            [
                rotate(grad_queries, cos_table, -sin_table, ROT),
                rotate(grad_keys, cos_table, -sin_table, ROT),
                grad_values,
            ],
            axis=1,
        )
        grad_projected = grad_projected.reshape(group_rows, 3, local_cols).astype(bf16)
        attend_bias_grad = jnp.sum(grad_projected.astype(f32), axis=0)
        attend_grad = jnp.einsum("td,tcn->dcn", branch_one, grad_projected, preferred_element_type=f32)
        grad_one = jnp.einsum("tcn,dcn->td", grad_projected, attend_full, preferred_element_type=f32)

        attend_bias_parts = (
            attend_bias_grad.reshape(3, dp_count, attend_bias.shape[1])
            .transpose(1, 0, 2)
            .reshape(dp_count, -1)
        )
        attn_payload = lane_rows(
            [attend_grad.reshape(dp_count, -1), output_grad.reshape(dp_count, -1), attend_bias_parts],
            axis=1,
        ).astype(bf16)
        expand_full, shrink_parts, _ = lax.optimization_barrier(
            (expand_full, shrink_parts, attn_payload)
        )

        expanded = jnp.dot(
            branch_two, expand_full, preferred_element_type=f32
        ) + expand_bias_full.astype(f32)
        activated, gelu_back = jax.vjp(lambda value: jax.nn.gelu(value, approximate=False), expanded)
        activated_low = activated.astype(bf16)
        ffn_out = jnp.einsum(
            "tf,kfe->tke", activated_low, shrink_parts, preferred_element_type=f32
        ).reshape(group_rows, width)
        grad_activated = jnp.einsum(
            "tke,kfe->tf", grad_rows_parts, shrink_parts, preferred_element_type=f32
        )
        shrink_grad = jnp.einsum(
            "tf,tke->kfe", activated_low, grad_rows_parts, preferred_element_type=f32
        )
        grad_expanded = gelu_back(grad_activated)[0].astype(bf16)
        expand_bias_grad = jnp.sum(grad_expanded.astype(f32), axis=0)
        expand_grad = jnp.einsum("td,tf->df", branch_two, grad_expanded, preferred_element_type=f32)
        grad_two = jnp.einsum("tf,df->td", grad_expanded, expand_full, preferred_element_type=f32)
        out_bias_sum = jnp.sum(grad_rows.astype(f32), axis=0).reshape(dp_count, tp_count, piece)
        out_bias_mine = lax.dynamic_index_in_dim(out_bias_sum, tensor_index, axis=1, keepdims=False)

        partial_out = ffn_out + attn_out

        norm_partials = jnp.stack(
            [
                jnp.sum(grad_one * standard, axis=0),
                jnp.sum(grad_one, axis=0),
                jnp.sum(grad_two * standard, axis=0),
                jnp.sum(grad_two, axis=0),
            ]
        )
        scaled_parts = grad_one * gain_one + grad_two * gain_two
        token_parts = jnp.concatenate([partial_out, scaled_parts], axis=1).reshape(
            tp_count, local_rows, 2 * width
        )
        reduced = ring_reduce(token_parts.astype(bf16), "tensor", tp_count, tensor_index)
        summed = reduced[:, :width]
        scaled = reduced[:, width:]
        attn_reduced = lax.psum_scatter(attn_payload, "dp", scatter_dimension=0, tiled=True)
        ffn_payload = lane_rows(
            [
                expand_grad.reshape(dp_count, -1),
                shrink_grad.reshape(dp_count, -1),
                expand_bias_grad.reshape(dp_count, -1),
                out_bias_mine,
                norm_partials.reshape(4, dp_count, -1).transpose(1, 0, 2).reshape(dp_count, -1),
            ],
            axis=1,
        ).astype(bf16)
        attn_reduced, ffn_payload = lax.optimization_barrier((attn_reduced, ffn_payload))
        attn_grads = attn_reduced.reshape(-1).astype(f32)
        at = 0
        attend_weight_grad = attn_grads[at : at + attend_weight.size].reshape(attend_weight.shape)
        at += -(-attend_weight.size // 128) * 128
        output_weight_grad = attn_grads[at : at + output_weight.size].reshape(output_weight.shape)
        at += -(-output_weight.size // 128) * 128
        attend_bias_out = attn_grads[at : at + attend_bias.size].reshape(attend_bias.shape)


        ffn_grads = lax.psum_scatter(
            ffn_payload,
            "dp",
            scatter_dimension=0,
            tiled=True,
        ).reshape(-1).astype(f32)
        at = 0
        expand_weight_grad = ffn_grads[at : at + expand_weight.size].reshape(expand_weight.shape)
        at += -(-expand_weight.size // 128) * 128
        shrink_weight_grad = ffn_grads[at : at + shrink_weight.size].reshape(shrink_weight.shape)
        at += -(-shrink_weight.size // 128) * 128
        expand_bias_out = ffn_grads[at : at + expand_bias.size]
        at += -(-expand_bias.size // 128) * 128
        out_bias_grad = ffn_grads[at : at + piece]
        at += -(-piece // 128) * 128
        norm_grads = ring_reduce(
            ffn_grads[at : at + 4 * tp_count * piece].reshape(4, tp_count, piece).transpose(1, 0, 2),
            "tensor",
            tp_count,
            tensor_index,
        )

        hidden_out = (hidden_in.astype(f32) + summed + out_bias_full + shrink_bias_full).astype(bf16)
        start = tensor_index * local_rows
        standard_local = lax.dynamic_slice_in_dim(standard, start, local_rows, 0)
        inverse_local = lax.dynamic_slice_in_dim(inverse_std, start, local_rows, 0)
        input_grad = cotangent.astype(f32) + norm_backward(scaled, standard_local, inverse_local)
        return (
            hidden_out,
            input_grad,
            norm_grads[0],
            norm_grads[1],
            norm_grads[2],
            norm_grads[3],
            attend_weight_grad,
            attend_bias_out,
            output_weight_grad,
            out_bias_grad,
            expand_weight_grad,
            expand_bias_out,
            shrink_weight_grad,
            out_bias_grad,
        )
    in_specs = (
        P(("dp", "tensor"), None),
        P(("dp", "tensor"), None),
        P("dp", None),
        P("dp"),
        P(("dp", "tensor")),
        P(("dp", "tensor")),
        P(("dp", "tensor")),
        P(("dp", "tensor")),
        P("dp", None, "tensor"),
        P(None, ("tensor", "dp")),
        P("tensor", "dp"),
        P(("dp", "tensor")),
        P("dp", "tensor"),
        P(("tensor", "dp")),
        P("tensor", "dp"),
        P(("dp", "tensor")),
    )
    out_specs = (
        P(("dp", "tensor"), None),
        P(("dp", "tensor"), None),
        P(("dp", "tensor")),
        P(("dp", "tensor")),
        P(("dp", "tensor")),
        P(("dp", "tensor")),
        P("dp", None, "tensor"),
        P(None, ("tensor", "dp")),
        P("tensor", "dp"),
        P(("dp", "tensor")),
        P("dp", "tensor"),
        P(("tensor", "dp")),
        P("tensor", "dp"),
        P(("dp", "tensor")),
    )
    return jax.shard_map(
        per_device, mesh=mesh, in_specs=in_specs, out_specs=out_specs, check_vma=False
    )
```

```python
import jax
import jax.numpy as jnp
from jax import lax
from jax.sharding import PartitionSpec as P

HD = 64
ROT = 16


EPSILON = 1e-05
NEGATIVE = -1000000000.0


def rotate(tensor, cos_table, sin_table, rot_dims):
    half_dims = rot_dims // 2
    lower_half = tensor[..., :half_dims]
    upper_half = tensor[..., half_dims:rot_dims]
    return jnp.concatenate(
        [
            lower_half * cos_table - upper_half * sin_table,
            upper_half * cos_table + lower_half * sin_table,
            tensor[..., rot_dims:],
        ],
        axis=-1,
    )


def norm_backward(scaled, standard, inverse_std):
    mean_scaled = jnp.mean(scaled, axis=-1, keepdims=True)
    mean_cross = jnp.mean(scaled * standard, axis=-1, keepdims=True)
    return inverse_std * (scaled - mean_scaled - standard * mean_cross)


def lane_rows(parts, axis=1):
    padded = []
    for part in parts:
        extra = -part.shape[1] % 128
        padded.append(jnp.pad(part, ((0, 0), (0, extra))))
    joined = jnp.concatenate(padded, axis=axis)
    joined = joined.reshape(joined.shape[0], -1, 128)
    joined = jnp.pad(joined, ((0, 0), (0, -joined.shape[1] % 16), (0, 0)))
    return joined.reshape(-1, 128)


def gather_rows(parts, axis, permute_with=None):
    flat, offsets, at = [], [], 0
    for part in parts:
        part = part.reshape(-1)
        extra = -part.shape[0] % 128
        flat.append(jnp.pad(part, (0, extra)))
        offsets.append(at)
        at += part.shape[0] + extra
    joined = jnp.concatenate(flat).reshape(-1, 128)
    joined = jnp.pad(joined, ((0, -joined.shape[0] % 16), (0, 0)))
    if permute_with is None:
        gathered = lax.all_gather(joined, axis, axis=0)
    else:
        gathered = ring_gather(joined, axis, *permute_with)
    return gathered.reshape(gathered.shape[0], -1), offsets


def ring_gather(block, axis, count, index):
    parts = [block] + [
        lax.ppermute(block, axis, [(j, (j + k) % count) for j in range(count)])
        for k in range(1, count)
    ]
    backward = jnp.stack([parts[0]] + parts[:0:-1])
    doubled = jnp.concatenate([backward, backward])
    return lax.dynamic_slice_in_dim(doubled, (count - index) % count, count, 0)


def ring_reduce(chunks, axis, count, index):
    total = lax.dynamic_index_in_dim(chunks, index, 0, keepdims=False).astype(jnp.float32)
    for k in range(1, count):
        send = lax.dynamic_index_in_dim(chunks, (index + k) % count, 0, keepdims=False)
        moved = lax.ppermute(send, axis, [(j, (j + k) % count) for j in range(count)])
        total = total + moved.astype(jnp.float32)
    return total


def solution(mesh):
    dp_count = mesh.shape["dp"]
    tp_count = mesh.shape["tensor"]

    def per_device(
        hidden_in,
        cotangent,
        segment_ids,
        live_count,
        first_gain,
        first_bias,
        second_gain,
        second_bias,
        attend_weight,
        attend_bias,
        output_weight,
        output_bias,
        expand_weight,
        expand_bias,
        shrink_weight,
        shrink_bias,
    ):
        f32 = jnp.float32
        bf16 = jnp.bfloat16
        local_rows, width = hidden_in.shape
        group_rows = local_rows * tp_count
        piece = first_gain.shape[0]
        dp_rows, _, local_cols = attend_weight.shape
        local_ff = expand_weight.shape[1]
        tensor_index = lax.axis_index("tensor")

        small = jnp.concatenate(
            [
                first_gain,
                first_bias,
                second_gain,
                second_bias,
                output_bias,
                shrink_bias,
                attend_bias.reshape(-1),
                expand_bias,
            ]
        )
        small_len = small.shape[0]
        gathered = ring_gather(
            jnp.concatenate([hidden_in, cotangent], axis=0), "tensor", tp_count, tensor_index
        )
        rows_all = gathered[:, :local_rows].reshape(group_rows, width)
        grad_rows = gathered[:, local_rows:].reshape(group_rows, width)

        attend_all, (attend_at, output_at, small_at) = gather_rows(
            [attend_weight, output_weight, small],
            "dp",
            (dp_count, lax.axis_index("dp")) if dp_count <= 8 else None,
        )
        attend_full = attend_all[:, attend_at : attend_at + attend_weight.size].reshape(
            dp_count * dp_rows, 3, local_cols
        )
        output_parts = attend_all[:, output_at : output_at + output_weight.size].reshape(
            dp_count, local_cols, dp_rows
        )
        small_all = ring_gather(
            attend_all[:, small_at : small_at + small_len], "tensor", tp_count, tensor_index
        ).transpose(1, 0, 2)

        def full_vector(k):
            return small_all[:, :, k * piece : (k + 1) * piece].reshape(-1).astype(f32)

        gain_one, bias_one, gain_two, bias_two, out_bias_full, shrink_bias_full = [
            full_vector(k) for k in range(6)
        ]
        small_mine = lax.dynamic_index_in_dim(small_all, tensor_index, axis=1, keepdims=False)
        attend_bias_full = (
            small_mine[:, 6 * piece : 6 * piece + attend_bias.size]
            .reshape(dp_count, 3, attend_bias.shape[1])
            .transpose(1, 0, 2)
            .reshape(3, local_cols)
        )
        expand_bias_full = small_mine[:, 6 * piece + attend_bias.size :].reshape(-1)

        ffn_all, (expand_at, shrink_at) = gather_rows([expand_weight, shrink_weight], "dp")
        expand_full = ffn_all[:, expand_at : expand_at + expand_weight.size].reshape(
            dp_count * dp_rows, local_ff
        )
        shrink_parts = ffn_all[:, shrink_at : shrink_at + shrink_weight.size].reshape(
            dp_count, local_ff, dp_rows
        )

        local_heads = local_cols // HD
        scale = HD ** (-0.5)
        rows_float = rows_all.astype(f32)
        centre = rows_float - jnp.mean(rows_float, axis=-1, keepdims=True)
        inverse_std = lax.rsqrt(jnp.mean(centre * centre, axis=-1, keepdims=True) + EPSILON)
        standard = centre * inverse_std
        branch_one = (standard * gain_one + bias_one).astype(bf16)
        branch_two = (standard * gain_two + bias_two).astype(bf16)
        grad_rows_parts = grad_rows.reshape(group_rows, dp_count, dp_rows)

        projected = (
            jnp.einsum("td,dcn->tcn", branch_one, attend_full, preferred_element_type=f32)
            + attend_bias_full.astype(f32)[None]
        )
        segments = segment_ids[0]
        index = jnp.arange(group_rows)
        same_seq = segments[:, None] == segments[None, :]
        positions = jnp.sum((same_seq & (index[None, :] < index[:, None])).astype(f32), axis=1)
        allowed = (
            same_seq
            & (index[None, :] <= index[:, None])
            & ((index[None, :] < live_count[0]) | (index[None, :] == index[:, None]))
        )
        half_dims = ROT // 2
        inverse = 10000.0 ** (-jnp.arange(half_dims).astype(f32) * 2.0 / ROT)
        angles = positions[:, None] * inverse[None, :]
        cos_table = jnp.cos(angles)[:, None, :]
        sin_table = jnp.sin(angles)[:, None, :]
        per_head = projected.reshape(group_rows, 3, local_heads, HD)
        queries = rotate(per_head[:, 0], cos_table, sin_table, ROT).astype(bf16)
        keys_rot = rotate(per_head[:, 1], cos_table, sin_table, ROT).astype(bf16)
        values = per_head[:, 2].astype(bf16)
        scores = jnp.einsum("thd,uhd->htu", queries, keys_rot, preferred_element_type=f32) * scale
        scores = jnp.where(allowed[None], scores, NEGATIVE)
        top_score = jnp.max(scores, axis=-1, keepdims=True)
        log_total = top_score + jnp.log(jnp.sum(jnp.exp(scores - top_score), axis=-1, keepdims=True))
        probs = jnp.exp(scores - log_total)
        mixed = jnp.einsum("htu,uhd->thd", probs.astype(bf16), values, preferred_element_type=f32)
        mixed = mixed.reshape(group_rows, local_heads * HD).astype(bf16)
        attn_out = jnp.einsum(
            "tn,kne->tke", mixed, output_parts, preferred_element_type=f32
        ).reshape(group_rows, width)

        grad_mixed = jnp.einsum(
            "tke,kne->tn", grad_rows_parts, output_parts, preferred_element_type=f32
        ).astype(bf16)
        output_grad = jnp.einsum("tn,tke->kne", mixed, grad_rows_parts, preferred_element_type=f32)
        grad_mixed = grad_mixed.reshape(group_rows, local_heads, HD)
        probs_again = jnp.where(allowed[None], probs, 0.0)
        grad_values = jnp.einsum(
            "htu,thd->uhd", probs_again.astype(bf16), grad_mixed, preferred_element_type=f32
        )
        grad_probs = jnp.einsum("thd,uhd->htu", grad_mixed, values, preferred_element_type=f32)
        row_cross = jnp.sum(grad_probs * probs_again, axis=-1, keepdims=True)
        grad_scores = (probs_again * (grad_probs - row_cross)).astype(bf16)
        grad_queries = (
            jnp.einsum("htu,uhd->thd", grad_scores, keys_rot, preferred_element_type=f32) * scale
        )
        grad_keys = jnp.einsum("htu,thd->uhd", grad_scores, queries, preferred_element_type=f32) * scale
        grad_projected = jnp.stack(
            [
                rotate(grad_queries, cos_table, -sin_table, ROT),
                rotate(grad_keys, cos_table, -sin_table, ROT),
                grad_values,
            ],
            axis=1,
        )
        grad_projected = grad_projected.reshape(group_rows, 3, local_cols).astype(bf16)
        attend_bias_grad = jnp.sum(grad_projected.astype(f32), axis=0)
        attend_grad = jnp.einsum("td,tcn->dcn", branch_one, grad_projected, preferred_element_type=f32)
        grad_one = jnp.einsum("tcn,dcn->td", grad_projected, attend_full, preferred_element_type=f32)

        attend_bias_parts = (
            attend_bias_grad.reshape(3, dp_count, attend_bias.shape[1])
            .transpose(1, 0, 2)
            .reshape(dp_count, -1)
        )
        attn_payload = lane_rows(
            [attend_grad.reshape(dp_count, -1), output_grad.reshape(dp_count, -1), attend_bias_parts],
            axis=1,
        ).astype(bf16)
        expand_full, shrink_parts, _ = lax.optimization_barrier(
            (expand_full, shrink_parts, attn_payload)
        )

        expanded = jnp.dot(
            branch_two, expand_full, preferred_element_type=f32
        ) + expand_bias_full.astype(f32)
        activated, gelu_back = jax.vjp(lambda value: jax.nn.gelu(value, approximate=False), expanded)
        activated_low = activated.astype(bf16)
        ffn_out = jnp.einsum(
            "tf,kfe->tke", activated_low, shrink_parts, preferred_element_type=f32
        ).reshape(group_rows, width)
        grad_activated = jnp.einsum(
            "tke,kfe->tf", grad_rows_parts, shrink_parts, preferred_element_type=f32
        )
        shrink_grad = jnp.einsum(
            "tf,tke->kfe", activated_low, grad_rows_parts, preferred_element_type=f32
        )
        grad_expanded = gelu_back(grad_activated)[0].astype(bf16)
        expand_bias_grad = jnp.sum(grad_expanded.astype(f32), axis=0)
        expand_grad = jnp.einsum("td,tf->df", branch_two, grad_expanded, preferred_element_type=f32)
        grad_two = jnp.einsum("tf,df->td", grad_expanded, expand_full, preferred_element_type=f32)
        out_bias_sum = jnp.sum(grad_rows.astype(f32), axis=0).reshape(dp_count, tp_count, piece)
        out_bias_mine = lax.dynamic_index_in_dim(out_bias_sum, tensor_index, axis=1, keepdims=False)

        partial_out = ffn_out + attn_out

        norm_partials = jnp.stack(
            [
                jnp.sum(grad_one * standard, axis=0),
                jnp.sum(grad_one, axis=0),
                jnp.sum(grad_two * standard, axis=0),
                jnp.sum(grad_two, axis=0),
            ]
        )
        scaled_parts = grad_one * gain_one + grad_two * gain_two
        token_parts = jnp.concatenate([partial_out, scaled_parts], axis=1).reshape(
            tp_count, local_rows, 2 * width
        )
        reduced = ring_reduce(token_parts.astype(bf16), "tensor", tp_count, tensor_index)
        summed = reduced[:, :width]
        scaled = reduced[:, width:]
        attn_reduced = lax.psum_scatter(attn_payload, "dp", scatter_dimension=0, tiled=True)
        ffn_payload = lane_rows(
            [
                expand_grad.reshape(dp_count, -1),
                shrink_grad.reshape(dp_count, -1),
                expand_bias_grad.reshape(dp_count, -1),
                out_bias_mine,
                norm_partials.reshape(4, dp_count, -1).transpose(1, 0, 2).reshape(dp_count, -1),
            ],
            axis=1,
        ).astype(bf16)
        attn_reduced, ffn_payload = lax.optimization_barrier((attn_reduced, ffn_payload))
        attn_grads = attn_reduced.reshape(-1).astype(f32)
        at = 0
        attend_weight_grad = attn_grads[at : at + attend_weight.size].reshape(attend_weight.shape)
        at += -(-attend_weight.size // 128) * 128
        output_weight_grad = attn_grads[at : at + output_weight.size].reshape(output_weight.shape)
        at += -(-output_weight.size // 128) * 128
        attend_bias_out = attn_grads[at : at + attend_bias.size].reshape(attend_bias.shape)


        ffn_grads = lax.psum_scatter(
            ffn_payload,
            "dp",
            scatter_dimension=0,
            tiled=True,
        ).reshape(-1).astype(f32)
        at = 0
        expand_weight_grad = ffn_grads[at : at + expand_weight.size].reshape(expand_weight.shape)
        at += -(-expand_weight.size // 128) * 128
        shrink_weight_grad = ffn_grads[at : at + shrink_weight.size].reshape(shrink_weight.shape)
        at += -(-shrink_weight.size // 128) * 128
        expand_bias_out = ffn_grads[at : at + expand_bias.size]
        at += -(-expand_bias.size // 128) * 128
        out_bias_grad = ffn_grads[at : at + piece]
        at += -(-piece // 128) * 128
        norm_grads = ring_reduce(
            ffn_grads[at : at + 4 * tp_count * piece].reshape(4, tp_count, piece).transpose(1, 0, 2),
            "tensor",
            tp_count,
            tensor_index,
        )

        hidden_out = (hidden_in.astype(f32) + summed + out_bias_full + shrink_bias_full).astype(bf16)
        start = tensor_index * local_rows
        standard_local = lax.dynamic_slice_in_dim(standard, start, local_rows, 0)
        inverse_local = lax.dynamic_slice_in_dim(inverse_std, start, local_rows, 0)
        input_grad = cotangent.astype(f32) + norm_backward(scaled, standard_local, inverse_local)
        return (
            hidden_out,
            input_grad,
            norm_grads[0],
            norm_grads[1],
            norm_grads[2],
            norm_grads[3],
            attend_weight_grad,
            attend_bias_out,
            output_weight_grad,
            out_bias_grad,
            expand_weight_grad,
            expand_bias_out,
            shrink_weight_grad,
            out_bias_grad,
        )
    in_specs = (
        P(("dp", "tensor"), None),
        P(("dp", "tensor"), None),
        P("dp", None),
        P("dp"),
        P(("dp", "tensor")),
        P(("dp", "tensor")),
        P(("dp", "tensor")),
        P(("dp", "tensor")),
        P("dp", None, "tensor"),
        P(None, ("tensor", "dp")),
        P("tensor", "dp"),
        P(("dp", "tensor")),
        P("dp", "tensor"),
        P(("tensor", "dp")),
        P("tensor", "dp"),
        P(("dp", "tensor")),
    )
    out_specs = (
        P(("dp", "tensor"), None),
        P(("dp", "tensor"), None),
        P(("dp", "tensor")),
        P(("dp", "tensor")),
        P(("dp", "tensor")),
        P(("dp", "tensor")),
        P("dp", None, "tensor"),
        P(None, ("tensor", "dp")),
        P("tensor", "dp"),
        P(("dp", "tensor")),
        P("dp", "tensor"),
        P(("tensor", "dp")),
        P("tensor", "dp"),
        P(("dp", "tensor")),
    )
    return jax.shard_map(
        per_device, mesh=mesh, in_specs=in_specs, out_specs=out_specs, check_vma=False
    )
```

```python
import jax
import jax.numpy as jnp
from jax import lax
from jax.sharding import PartitionSpec as P

HD = 64
ROT = 16


EPSILON = 1e-05
NEGATIVE = -1000000000.0


def rotate(tensor, cos_table, sin_table, rot_dims):
    half_dims = rot_dims // 2
    lower_half = tensor[..., :half_dims]
    upper_half = tensor[..., half_dims:rot_dims]
    return jnp.concatenate(
        [
            lower_half * cos_table - upper_half * sin_table,
            upper_half * cos_table + lower_half * sin_table,
            tensor[..., rot_dims:],
        ],
        axis=-1,
    )


def norm_backward(scaled, standard, inverse_std):
    mean_scaled = jnp.mean(scaled, axis=-1, keepdims=True)
    mean_cross = jnp.mean(scaled * standard, axis=-1, keepdims=True)
    return inverse_std * (scaled - mean_scaled - standard * mean_cross)


def lane_rows(parts, axis=1):
    padded = []
    for part in parts:
        extra = -part.shape[1] % 128
        padded.append(jnp.pad(part, ((0, 0), (0, extra))))
    joined = jnp.concatenate(padded, axis=axis)
    joined = joined.reshape(joined.shape[0], -1, 128)
    joined = jnp.pad(joined, ((0, 0), (0, -joined.shape[1] % 16), (0, 0)))
    return joined.reshape(-1, 128)


def ring_neighbour_gather(block, axis, order, index):
    count = len(order)
    position_of = [order.index(d) for d in range(count)]
    ahead = [(order[p], order[(p + 1) % count]) for p in range(count)]
    behind = [(order[p], order[(p - 1) % count]) for p in range(count)]
    half = block.shape[0] // 2
    moving_a, moving_b = block[:half], block[half:]
    got_a, got_b = [moving_a], [moving_b]
    for _ in range(1, count):
        moving_a = lax.ppermute(moving_a, axis, ahead)
        moving_b = lax.ppermute(moving_b, axis, behind)
        got_a.append(moving_a)
        got_b.append(moving_b)
    mine = jnp.asarray(position_of, jnp.int32)[index]
    backward = jnp.stack([got_a[0]] + got_a[:0:-1])
    by_ring_a = lax.dynamic_slice_in_dim(
        jnp.concatenate([backward, backward]), (count - mine) % count, count, 0
    )
    forward = jnp.stack(got_b)
    by_ring_b = lax.dynamic_slice_in_dim(
        jnp.concatenate([forward, forward]), (count - mine) % count, count, 0
    )
    by_ring = jnp.concatenate([by_ring_a, by_ring_b], axis=1)
    return jnp.stack([by_ring[position_of[d]] for d in range(count)])


def gather_rows(parts, axis, ring=None):
    flat, offsets, at = [], [], 0
    for part in parts:
        part = part.reshape(-1)
        extra = -part.shape[0] % 128
        flat.append(jnp.pad(part, (0, extra)))
        offsets.append(at)
        at += part.shape[0] + extra
    joined = jnp.concatenate(flat).reshape(-1, 128)
    joined = jnp.pad(joined, ((0, -joined.shape[0] % 16), (0, 0)))
    if ring is None:
        gathered = lax.all_gather(joined, axis, axis=0)
    else:
        gathered = ring_neighbour_gather(joined, axis, *ring)
    return gathered.reshape(gathered.shape[0], -1), offsets


def ring_gather(block, axis, count, index):
    parts = [block] + [
        lax.ppermute(block, axis, [(j, (j + k) % count) for j in range(count)])
        for k in range(1, count)
    ]
    backward = jnp.stack([parts[0]] + parts[:0:-1])
    doubled = jnp.concatenate([backward, backward])
    return lax.dynamic_slice_in_dim(doubled, (count - index) % count, count, 0)


def ring_reduce(chunks, axis, count, index):
    total = lax.dynamic_index_in_dim(chunks, index, 0, keepdims=False).astype(jnp.float32)
    for k in range(1, count):
        send = lax.dynamic_index_in_dim(chunks, (index + k) % count, 0, keepdims=False)
        moved = lax.ppermute(send, axis, [(j, (j + k) % count) for j in range(count)])
        total = total + moved.astype(jnp.float32)
    return total


def solution(mesh):
    dp_count = mesh.shape["dp"]
    tp_count = mesh.shape["tensor"]

    def per_device(
        hidden_in,
        cotangent,
        segment_ids,
        live_count,
        first_gain,
        first_bias,
        second_gain,
        second_bias,
        attend_weight,
        attend_bias,
        output_weight,
        output_bias,
        expand_weight,
        expand_bias,
        shrink_weight,
        shrink_bias,
    ):
        f32 = jnp.float32
        bf16 = jnp.bfloat16
        local_rows, width = hidden_in.shape
        group_rows = local_rows * tp_count
        piece = first_gain.shape[0]
        dp_rows, _, local_cols = attend_weight.shape
        local_ff = expand_weight.shape[1]
        tensor_index = lax.axis_index("tensor")

        small = jnp.concatenate(
            [
                first_gain,
                first_bias,
                second_gain,
                second_bias,
                output_bias,
                shrink_bias,
                attend_bias.reshape(-1),
                expand_bias,
            ]
        )
        small_len = small.shape[0]
        gathered = ring_gather(
            jnp.concatenate([hidden_in, cotangent], axis=0), "tensor", tp_count, tensor_index
        )
        rows_all = gathered[:, :local_rows].reshape(group_rows, width)
        grad_rows = gathered[:, local_rows:].reshape(group_rows, width)

        attend_all, (attend_at, output_at, small_at) = gather_rows(
            [attend_weight, output_weight, small],
            "dp",
            ((0, 2, 4, 6, 7, 5, 3, 1), lax.axis_index("dp")) if dp_count == 8 else None,
        )
        attend_full = attend_all[:, attend_at : attend_at + attend_weight.size].reshape(
            dp_count * dp_rows, 3, local_cols
        )
        output_parts = attend_all[:, output_at : output_at + output_weight.size].reshape(
            dp_count, local_cols, dp_rows
        )
        small_all = ring_gather(
            attend_all[:, small_at : small_at + small_len], "tensor", tp_count, tensor_index
        ).transpose(1, 0, 2)

        def full_vector(k):
            return small_all[:, :, k * piece : (k + 1) * piece].reshape(-1).astype(f32)

        gain_one, bias_one, gain_two, bias_two, out_bias_full, shrink_bias_full = [
            full_vector(k) for k in range(6)
        ]
        small_mine = lax.dynamic_index_in_dim(small_all, tensor_index, axis=1, keepdims=False)
        attend_bias_full = (
            small_mine[:, 6 * piece : 6 * piece + attend_bias.size]
            .reshape(dp_count, 3, attend_bias.shape[1])
            .transpose(1, 0, 2)
            .reshape(3, local_cols)
        )
        expand_bias_full = small_mine[:, 6 * piece + attend_bias.size :].reshape(-1)

        ffn_all, (expand_at, shrink_at) = gather_rows([expand_weight, shrink_weight], "dp")
        expand_full = ffn_all[:, expand_at : expand_at + expand_weight.size].reshape(
            dp_count * dp_rows, local_ff
        )
        shrink_parts = ffn_all[:, shrink_at : shrink_at + shrink_weight.size].reshape(
            dp_count, local_ff, dp_rows
        )

        local_heads = local_cols // HD
        scale = HD ** (-0.5)
        rows_float = rows_all.astype(f32)
        centre = rows_float - jnp.mean(rows_float, axis=-1, keepdims=True)
        inverse_std = lax.rsqrt(jnp.mean(centre * centre, axis=-1, keepdims=True) + EPSILON)
        standard = centre * inverse_std
        branch_one = (standard * gain_one + bias_one).astype(bf16)
        branch_two = (standard * gain_two + bias_two).astype(bf16)
        grad_rows_parts = grad_rows.reshape(group_rows, dp_count, dp_rows)

        projected = (
            jnp.einsum("td,dcn->tcn", branch_one, attend_full, preferred_element_type=f32)
            + attend_bias_full.astype(f32)[None]
        )
        segments = segment_ids[0]
        index = jnp.arange(group_rows)
        same_seq = segments[:, None] == segments[None, :]
        positions = jnp.sum((same_seq & (index[None, :] < index[:, None])).astype(f32), axis=1)
        allowed = (
            same_seq
            & (index[None, :] <= index[:, None])
            & ((index[None, :] < live_count[0]) | (index[None, :] == index[:, None]))
        )
        half_dims = ROT // 2
        inverse = 10000.0 ** (-jnp.arange(half_dims).astype(f32) * 2.0 / ROT)
        angles = positions[:, None] * inverse[None, :]
        cos_table = jnp.cos(angles)[:, None, :]
        sin_table = jnp.sin(angles)[:, None, :]
        per_head = projected.reshape(group_rows, 3, local_heads, HD)
        queries = rotate(per_head[:, 0], cos_table, sin_table, ROT).astype(bf16)
        keys_rot = rotate(per_head[:, 1], cos_table, sin_table, ROT).astype(bf16)
        values = per_head[:, 2].astype(bf16)
        scores = jnp.einsum("thd,uhd->htu", queries, keys_rot, preferred_element_type=f32) * scale
        scores = jnp.where(allowed[None], scores, NEGATIVE)
        top_score = jnp.max(scores, axis=-1, keepdims=True)
        log_total = top_score + jnp.log(jnp.sum(jnp.exp(scores - top_score), axis=-1, keepdims=True))
        probs = jnp.exp(scores - log_total)
        mixed = jnp.einsum("htu,uhd->thd", probs.astype(bf16), values, preferred_element_type=f32)
        mixed = mixed.reshape(group_rows, local_heads * HD).astype(bf16)
        attn_out = jnp.einsum(
            "tn,kne->tke", mixed, output_parts, preferred_element_type=f32
        ).reshape(group_rows, width)

        grad_mixed = jnp.einsum(
            "tke,kne->tn", grad_rows_parts, output_parts, preferred_element_type=f32
        ).astype(bf16)
        output_grad = jnp.einsum("tn,tke->kne", mixed, grad_rows_parts, preferred_element_type=f32)
        grad_mixed = grad_mixed.reshape(group_rows, local_heads, HD)
        probs_again = jnp.where(allowed[None], probs, 0.0)
        grad_values = jnp.einsum(
            "htu,thd->uhd", probs_again.astype(bf16), grad_mixed, preferred_element_type=f32
        )
        grad_probs = jnp.einsum("thd,uhd->htu", grad_mixed, values, preferred_element_type=f32)
        row_cross = jnp.sum(grad_probs * probs_again, axis=-1, keepdims=True)
        grad_scores = (probs_again * (grad_probs - row_cross)).astype(bf16)
        grad_queries = (
            jnp.einsum("htu,uhd->thd", grad_scores, keys_rot, preferred_element_type=f32) * scale
        )
        grad_keys = jnp.einsum("htu,thd->uhd", grad_scores, queries, preferred_element_type=f32) * scale
        grad_projected = jnp.stack(
            [
                rotate(grad_queries, cos_table, -sin_table, ROT),
                rotate(grad_keys, cos_table, -sin_table, ROT),
                grad_values,
            ],
            axis=1,
        )
        grad_projected = grad_projected.reshape(group_rows, 3, local_cols).astype(bf16)
        attend_bias_grad = jnp.sum(grad_projected.astype(f32), axis=0)
        attend_grad = jnp.einsum("td,tcn->dcn", branch_one, grad_projected, preferred_element_type=f32)
        grad_one = jnp.einsum("tcn,dcn->td", grad_projected, attend_full, preferred_element_type=f32)

        attend_bias_parts = (
            attend_bias_grad.reshape(3, dp_count, attend_bias.shape[1])
            .transpose(1, 0, 2)
            .reshape(dp_count, -1)
        )
        attn_payload = lane_rows(
            [attend_grad.reshape(dp_count, -1), output_grad.reshape(dp_count, -1), attend_bias_parts],
            axis=1,
        ).astype(bf16)
        expand_full, shrink_parts, _ = lax.optimization_barrier(
            (expand_full, shrink_parts, attn_payload)
        )

        expanded = jnp.dot(
            branch_two, expand_full, preferred_element_type=f32
        ) + expand_bias_full.astype(f32)
        activated, gelu_back = jax.vjp(lambda value: jax.nn.gelu(value, approximate=False), expanded)
        activated_low = activated.astype(bf16)
        ffn_out = jnp.einsum(
            "tf,kfe->tke", activated_low, shrink_parts, preferred_element_type=f32
        ).reshape(group_rows, width)
        grad_activated = jnp.einsum(
            "tke,kfe->tf", grad_rows_parts, shrink_parts, preferred_element_type=f32
        )
        shrink_grad = jnp.einsum(
            "tf,tke->kfe", activated_low, grad_rows_parts, preferred_element_type=f32
        )
        grad_expanded = gelu_back(grad_activated)[0].astype(bf16)
        expand_bias_grad = jnp.sum(grad_expanded.astype(f32), axis=0)
        expand_grad = jnp.einsum("td,tf->df", branch_two, grad_expanded, preferred_element_type=f32)
        grad_two = jnp.einsum("tf,df->td", grad_expanded, expand_full, preferred_element_type=f32)
        out_bias_sum = jnp.sum(grad_rows.astype(f32), axis=0).reshape(dp_count, tp_count, piece)
        out_bias_mine = lax.dynamic_index_in_dim(out_bias_sum, tensor_index, axis=1, keepdims=False)

        partial_out = ffn_out + attn_out

        norm_partials = jnp.stack(
            [
                jnp.sum(grad_one * standard, axis=0),
                jnp.sum(grad_one, axis=0),
                jnp.sum(grad_two * standard, axis=0),
                jnp.sum(grad_two, axis=0),
            ]
        )
        scaled_parts = grad_one * gain_one + grad_two * gain_two
        token_parts = jnp.concatenate([partial_out, scaled_parts], axis=1).reshape(
            tp_count, local_rows, 2 * width
        )
        reduced = ring_reduce(token_parts.astype(bf16), "tensor", tp_count, tensor_index)
        summed = reduced[:, :width]
        scaled = reduced[:, width:]
        attn_reduced = lax.psum_scatter(attn_payload, "dp", scatter_dimension=0, tiled=True)
        ffn_payload = lane_rows(
            [
                expand_grad.reshape(dp_count, -1),
                shrink_grad.reshape(dp_count, -1),
                expand_bias_grad.reshape(dp_count, -1),
                out_bias_mine,
                norm_partials.reshape(4, dp_count, -1).transpose(1, 0, 2).reshape(dp_count, -1),
            ],
            axis=1,
        ).astype(bf16)
        attn_reduced, ffn_payload = lax.optimization_barrier((attn_reduced, ffn_payload))
        attn_grads = attn_reduced.reshape(-1).astype(f32)
        at = 0
        attend_weight_grad = attn_grads[at : at + attend_weight.size].reshape(attend_weight.shape)
        at += -(-attend_weight.size // 128) * 128
        output_weight_grad = attn_grads[at : at + output_weight.size].reshape(output_weight.shape)
        at += -(-output_weight.size // 128) * 128
        attend_bias_out = attn_grads[at : at + attend_bias.size].reshape(attend_bias.shape)


        ffn_grads = lax.psum_scatter(
            ffn_payload,
            "dp",
            scatter_dimension=0,
            tiled=True,
        ).reshape(-1).astype(f32)
        at = 0
        expand_weight_grad = ffn_grads[at : at + expand_weight.size].reshape(expand_weight.shape)
        at += -(-expand_weight.size // 128) * 128
        shrink_weight_grad = ffn_grads[at : at + shrink_weight.size].reshape(shrink_weight.shape)
        at += -(-shrink_weight.size // 128) * 128
        expand_bias_out = ffn_grads[at : at + expand_bias.size]
        at += -(-expand_bias.size // 128) * 128
        out_bias_grad = ffn_grads[at : at + piece]
        at += -(-piece // 128) * 128
        norm_grads = ring_reduce(
            ffn_grads[at : at + 4 * tp_count * piece].reshape(4, tp_count, piece).transpose(1, 0, 2),
            "tensor",
            tp_count,
            tensor_index,
        )

        hidden_out = (hidden_in.astype(f32) + summed + out_bias_full + shrink_bias_full).astype(bf16)
        start = tensor_index * local_rows
        standard_local = lax.dynamic_slice_in_dim(standard, start, local_rows, 0)
        inverse_local = lax.dynamic_slice_in_dim(inverse_std, start, local_rows, 0)
        input_grad = cotangent.astype(f32) + norm_backward(scaled, standard_local, inverse_local)
        return (
            hidden_out,
            input_grad,
            norm_grads[0],
            norm_grads[1],
            norm_grads[2],
            norm_grads[3],
            attend_weight_grad,
            attend_bias_out,
            output_weight_grad,
            out_bias_grad,
            expand_weight_grad,
            expand_bias_out,
            shrink_weight_grad,
            out_bias_grad,
        )
    in_specs = (
        P(("dp", "tensor"), None),
        P(("dp", "tensor"), None),
        P("dp", None),
        P("dp"),
        P(("dp", "tensor")),
        P(("dp", "tensor")),
        P(("dp", "tensor")),
        P(("dp", "tensor")),
        P("dp", None, "tensor"),
        P(None, ("tensor", "dp")),
        P("tensor", "dp"),
        P(("dp", "tensor")),
        P("dp", "tensor"),
        P(("tensor", "dp")),
        P("tensor", "dp"),
        P(("dp", "tensor")),
    )
    out_specs = (
        P(("dp", "tensor"), None),
        P(("dp", "tensor"), None),
        P(("dp", "tensor")),
        P(("dp", "tensor")),
        P(("dp", "tensor")),
        P(("dp", "tensor")),
        P("dp", None, "tensor"),
        P(None, ("tensor", "dp")),
        P("tensor", "dp"),
        P(("dp", "tensor")),
        P("dp", "tensor"),
        P(("tensor", "dp")),
        P("tensor", "dp"),
        P(("dp", "tensor")),
    )
    return jax.shard_map(
        per_device, mesh=mesh, in_specs=in_specs, out_specs=out_specs, check_vma=False
    )
```

```python
import jax
import jax.numpy as jnp
from jax import lax
from jax.sharding import PartitionSpec as P

HD = 64
ROT = 16


EPSILON = 1e-05
NEGATIVE = -1000000000.0


def rotate(tensor, cos_table, sin_table, rot_dims):
    half_dims = rot_dims // 2
    lower_half = tensor[..., :half_dims]
    upper_half = tensor[..., half_dims:rot_dims]
    return jnp.concatenate(
        [
            lower_half * cos_table - upper_half * sin_table,
            upper_half * cos_table + lower_half * sin_table,
            tensor[..., rot_dims:],
        ],
        axis=-1,
    )


def norm_backward(scaled, standard, inverse_std):
    mean_scaled = jnp.mean(scaled, axis=-1, keepdims=True)
    mean_cross = jnp.mean(scaled * standard, axis=-1, keepdims=True)
    return inverse_std * (scaled - mean_scaled - standard * mean_cross)


def lane_rows(parts, axis=1):
    padded = []
    for part in parts:
        extra = -part.shape[1] % 128
        padded.append(jnp.pad(part, ((0, 0), (0, extra))))
    joined = jnp.concatenate(padded, axis=axis)
    joined = joined.reshape(joined.shape[0], -1, 128)
    joined = jnp.pad(joined, ((0, 0), (0, -joined.shape[1] % 16), (0, 0)))
    return joined.reshape(-1, 128)


def gather_rows(parts, axis):
    flat, offsets, at = [], [], 0
    for part in parts:
        part = part.reshape(-1)
        extra = -part.shape[0] % 128
        flat.append(jnp.pad(part, (0, extra)))
        offsets.append(at)
        at += part.shape[0] + extra
    joined = jnp.concatenate(flat).reshape(-1, 128)
    joined = jnp.pad(joined, ((0, -joined.shape[0] % 16), (0, 0)))
    gathered = lax.all_gather(joined, axis, axis=0)
    return gathered.reshape(gathered.shape[0], -1), offsets


def ring_gather(block, axis, count, index):
    parts = [block] + [
        lax.ppermute(block, axis, [(j, (j + k) % count) for j in range(count)])
        for k in range(1, count)
    ]
    backward = jnp.stack([parts[0]] + parts[:0:-1])
    doubled = jnp.concatenate([backward, backward])
    return lax.dynamic_slice_in_dim(doubled, (count - index) % count, count, 0)


def ring_reduce(chunks, axis, count, index):
    total = lax.dynamic_index_in_dim(chunks, index, 0, keepdims=False).astype(jnp.float32)
    for k in range(1, count):
        send = lax.dynamic_index_in_dim(chunks, (index + k) % count, 0, keepdims=False)
        moved = lax.ppermute(send, axis, [(j, (j + k) % count) for j in range(count)])
        total = total + moved.astype(jnp.float32)
    return total


def ring_neighbour_reduce(chunks, axis, order, index):
    count = len(order)
    position_of = [order.index(d) for d in range(count)]
    ahead = [(order[p], order[(p + 1) % count]) for p in range(count)]
    behind = [(order[p], order[(p - 1) % count]) for p in range(count)]
    half = chunks.shape[1] // 2
    by_ring = jnp.stack([chunks[order[q]] for q in range(count)])
    ring_a, ring_b = by_ring[:, :half], by_ring[:, half:]
    mine = jnp.asarray(position_of, jnp.int32)[index]

    def own(ring, at):
        return lax.dynamic_index_in_dim(ring, at % count, 0, keepdims=False).astype(jnp.float32)

    total_a = own(ring_a, mine - 1)
    total_b = own(ring_b, mine + 1)
    for step in range(1, count):
        moved_a = lax.ppermute(total_a.astype(chunks.dtype), axis, ahead)
        moved_b = lax.ppermute(total_b.astype(chunks.dtype), axis, behind)
        total_a = moved_a.astype(jnp.float32) + own(ring_a, mine - 1 - step)
        total_b = moved_b.astype(jnp.float32) + own(ring_b, mine + 1 + step)
    return jnp.concatenate([total_a, total_b], axis=0)


def solution(mesh):
    dp_count = mesh.shape["dp"]
    tp_count = mesh.shape["tensor"]

    def per_device(
        hidden_in,
        cotangent,
        segment_ids,
        live_count,
        first_gain,
        first_bias,
        second_gain,
        second_bias,
        attend_weight,
        attend_bias,
        output_weight,
        output_bias,
        expand_weight,
        expand_bias,
        shrink_weight,
        shrink_bias,
    ):
        f32 = jnp.float32
        bf16 = jnp.bfloat16
        local_rows, width = hidden_in.shape
        group_rows = local_rows * tp_count
        piece = first_gain.shape[0]
        dp_rows, _, local_cols = attend_weight.shape
        local_ff = expand_weight.shape[1]
        tensor_index = lax.axis_index("tensor")

        small = jnp.concatenate(
            [
                first_gain,
                first_bias,
                second_gain,
                second_bias,
                output_bias,
                shrink_bias,
                attend_bias.reshape(-1),
                expand_bias,
            ]
        )
        small_len = small.shape[0]
        gathered = ring_gather(
            jnp.concatenate([hidden_in, cotangent], axis=0), "tensor", tp_count, tensor_index
        )
        rows_all = gathered[:, :local_rows].reshape(group_rows, width)
        grad_rows = gathered[:, local_rows:].reshape(group_rows, width)

        attend_all, (attend_at, output_at, small_at) = gather_rows(
            [attend_weight, output_weight, small], "dp"
        )
        attend_full = attend_all[:, attend_at : attend_at + attend_weight.size].reshape(
            dp_count * dp_rows, 3, local_cols
        )
        output_parts = attend_all[:, output_at : output_at + output_weight.size].reshape(
            dp_count, local_cols, dp_rows
        )
        small_all = ring_gather(
            attend_all[:, small_at : small_at + small_len], "tensor", tp_count, tensor_index
        ).transpose(1, 0, 2)

        def full_vector(k):
            return small_all[:, :, k * piece : (k + 1) * piece].reshape(-1).astype(f32)

        gain_one, bias_one, gain_two, bias_two, out_bias_full, shrink_bias_full = [
            full_vector(k) for k in range(6)
        ]
        small_mine = lax.dynamic_index_in_dim(small_all, tensor_index, axis=1, keepdims=False)
        attend_bias_full = (
            small_mine[:, 6 * piece : 6 * piece + attend_bias.size]
            .reshape(dp_count, 3, attend_bias.shape[1])
            .transpose(1, 0, 2)
            .reshape(3, local_cols)
        )
        expand_bias_full = small_mine[:, 6 * piece + attend_bias.size :].reshape(-1)

        ffn_all, (expand_at, shrink_at) = gather_rows([expand_weight, shrink_weight], "dp")
        expand_full = ffn_all[:, expand_at : expand_at + expand_weight.size].reshape(
            dp_count * dp_rows, local_ff
        )
        shrink_parts = ffn_all[:, shrink_at : shrink_at + shrink_weight.size].reshape(
            dp_count, local_ff, dp_rows
        )

        local_heads = local_cols // HD
        scale = HD ** (-0.5)
        rows_float = rows_all.astype(f32)
        centre = rows_float - jnp.mean(rows_float, axis=-1, keepdims=True)
        inverse_std = lax.rsqrt(jnp.mean(centre * centre, axis=-1, keepdims=True) + EPSILON)
        standard = centre * inverse_std
        branch_one = (standard * gain_one + bias_one).astype(bf16)
        branch_two = (standard * gain_two + bias_two).astype(bf16)
        grad_rows_parts = grad_rows.reshape(group_rows, dp_count, dp_rows)

        projected = (
            jnp.einsum("td,dcn->tcn", branch_one, attend_full, preferred_element_type=f32)
            + attend_bias_full.astype(f32)[None]
        )
        segments = segment_ids[0]
        index = jnp.arange(group_rows)
        same_seq = segments[:, None] == segments[None, :]
        positions = jnp.sum((same_seq & (index[None, :] < index[:, None])).astype(f32), axis=1)
        allowed = (
            same_seq
            & (index[None, :] <= index[:, None])
            & ((index[None, :] < live_count[0]) | (index[None, :] == index[:, None]))
        )
        half_dims = ROT // 2
        inverse = 10000.0 ** (-jnp.arange(half_dims).astype(f32) * 2.0 / ROT)
        angles = positions[:, None] * inverse[None, :]
        cos_table = jnp.cos(angles)[:, None, :]
        sin_table = jnp.sin(angles)[:, None, :]
        per_head = projected.reshape(group_rows, 3, local_heads, HD)
        queries = rotate(per_head[:, 0], cos_table, sin_table, ROT).astype(bf16)
        keys_rot = rotate(per_head[:, 1], cos_table, sin_table, ROT).astype(bf16)
        values = per_head[:, 2].astype(bf16)
        scores = jnp.einsum("thd,uhd->htu", queries, keys_rot, preferred_element_type=f32) * scale
        scores = jnp.where(allowed[None], scores, NEGATIVE)
        top_score = jnp.max(scores, axis=-1, keepdims=True)
        log_total = top_score + jnp.log(jnp.sum(jnp.exp(scores - top_score), axis=-1, keepdims=True))
        probs = jnp.exp(scores - log_total)
        mixed = jnp.einsum("htu,uhd->thd", probs.astype(bf16), values, preferred_element_type=f32)
        mixed = mixed.reshape(group_rows, local_heads * HD).astype(bf16)
        attn_out = jnp.einsum(
            "tn,kne->tke", mixed, output_parts, preferred_element_type=f32
        ).reshape(group_rows, width)

        grad_mixed = jnp.einsum(
            "tke,kne->tn", grad_rows_parts, output_parts, preferred_element_type=f32
        ).astype(bf16)
        output_grad = jnp.einsum("tn,tke->kne", mixed, grad_rows_parts, preferred_element_type=f32)
        grad_mixed = grad_mixed.reshape(group_rows, local_heads, HD)
        probs_again = jnp.where(allowed[None], probs, 0.0)
        grad_values = jnp.einsum(
            "htu,thd->uhd", probs_again.astype(bf16), grad_mixed, preferred_element_type=f32
        )
        grad_probs = jnp.einsum("thd,uhd->htu", grad_mixed, values, preferred_element_type=f32)
        row_cross = jnp.sum(grad_probs * probs_again, axis=-1, keepdims=True)
        grad_scores = (probs_again * (grad_probs - row_cross)).astype(bf16)
        grad_queries = (
            jnp.einsum("htu,uhd->thd", grad_scores, keys_rot, preferred_element_type=f32) * scale
        )
        grad_keys = jnp.einsum("htu,thd->uhd", grad_scores, queries, preferred_element_type=f32) * scale
        grad_projected = jnp.stack(
            [
                rotate(grad_queries, cos_table, -sin_table, ROT),
                rotate(grad_keys, cos_table, -sin_table, ROT),
                grad_values,
            ],
            axis=1,
        )
        grad_projected = grad_projected.reshape(group_rows, 3, local_cols).astype(bf16)
        attend_bias_grad = jnp.sum(grad_projected.astype(f32), axis=0)
        attend_grad = jnp.einsum("td,tcn->dcn", branch_one, grad_projected, preferred_element_type=f32)
        grad_one = jnp.einsum("tcn,dcn->td", grad_projected, attend_full, preferred_element_type=f32)

        attend_bias_parts = (
            attend_bias_grad.reshape(3, dp_count, attend_bias.shape[1])
            .transpose(1, 0, 2)
            .reshape(dp_count, -1)
        )
        attn_payload = lane_rows(
            [attend_grad.reshape(dp_count, -1), output_grad.reshape(dp_count, -1), attend_bias_parts],
            axis=1,
        ).astype(bf16)
        expand_full, shrink_parts, _ = lax.optimization_barrier(
            (expand_full, shrink_parts, attn_payload)
        )

        expanded = jnp.dot(
            branch_two, expand_full, preferred_element_type=f32
        ) + expand_bias_full.astype(f32)
        activated, gelu_back = jax.vjp(lambda value: jax.nn.gelu(value, approximate=False), expanded)
        activated_low = activated.astype(bf16)
        ffn_out = jnp.einsum(
            "tf,kfe->tke", activated_low, shrink_parts, preferred_element_type=f32
        ).reshape(group_rows, width)
        grad_activated = jnp.einsum(
            "tke,kfe->tf", grad_rows_parts, shrink_parts, preferred_element_type=f32
        )
        shrink_grad = jnp.einsum(
            "tf,tke->kfe", activated_low, grad_rows_parts, preferred_element_type=f32
        )
        grad_expanded = gelu_back(grad_activated)[0].astype(bf16)
        expand_bias_grad = jnp.sum(grad_expanded.astype(f32), axis=0)
        expand_grad = jnp.einsum("td,tf->df", branch_two, grad_expanded, preferred_element_type=f32)
        grad_two = jnp.einsum("tf,df->td", grad_expanded, expand_full, preferred_element_type=f32)
        out_bias_sum = jnp.sum(grad_rows.astype(f32), axis=0).reshape(dp_count, tp_count, piece)
        out_bias_mine = lax.dynamic_index_in_dim(out_bias_sum, tensor_index, axis=1, keepdims=False)

        partial_out = ffn_out + attn_out

        norm_partials = jnp.stack(
            [
                jnp.sum(grad_one * standard, axis=0),
                jnp.sum(grad_one, axis=0),
                jnp.sum(grad_two * standard, axis=0),
                jnp.sum(grad_two, axis=0),
            ]
        )
        scaled_parts = grad_one * gain_one + grad_two * gain_two
        token_parts = jnp.concatenate([partial_out, scaled_parts], axis=1).reshape(
            tp_count, local_rows, 2 * width
        )
        reduced = ring_reduce(token_parts.astype(bf16), "tensor", tp_count, tensor_index)
        summed = reduced[:, :width]
        scaled = reduced[:, width:]
        if dp_count == 8:
            attn_reduced = ring_neighbour_reduce(
                attn_payload.reshape(dp_count, -1, 128),
                "dp",
                (0, 2, 4, 6, 7, 5, 3, 1),
                lax.axis_index("dp"),
            )
        else:
            attn_reduced = lax.psum_scatter(attn_payload, "dp", scatter_dimension=0, tiled=True)
        ffn_payload = lane_rows(
            [
                expand_grad.reshape(dp_count, -1),
                shrink_grad.reshape(dp_count, -1),
                expand_bias_grad.reshape(dp_count, -1),
                out_bias_mine,
                norm_partials.reshape(4, dp_count, -1).transpose(1, 0, 2).reshape(dp_count, -1),
            ],
            axis=1,
        ).astype(bf16)
        attn_grads = attn_reduced.reshape(-1).astype(f32)
        at = 0
        attend_weight_grad = attn_grads[at : at + attend_weight.size].reshape(attend_weight.shape)
        at += -(-attend_weight.size // 128) * 128
        output_weight_grad = attn_grads[at : at + output_weight.size].reshape(output_weight.shape)
        at += -(-output_weight.size // 128) * 128
        attend_bias_out = attn_grads[at : at + attend_bias.size].reshape(attend_bias.shape)


        ffn_grads = lax.psum_scatter(
            ffn_payload,
            "dp",
            scatter_dimension=0,
            tiled=True,
        ).reshape(-1).astype(f32)
        at = 0
        expand_weight_grad = ffn_grads[at : at + expand_weight.size].reshape(expand_weight.shape)
        at += -(-expand_weight.size // 128) * 128
        shrink_weight_grad = ffn_grads[at : at + shrink_weight.size].reshape(shrink_weight.shape)
        at += -(-shrink_weight.size // 128) * 128
        expand_bias_out = ffn_grads[at : at + expand_bias.size]
        at += -(-expand_bias.size // 128) * 128
        out_bias_grad = ffn_grads[at : at + piece]
        at += -(-piece // 128) * 128
        norm_grads = ring_reduce(
            ffn_grads[at : at + 4 * tp_count * piece].reshape(4, tp_count, piece).transpose(1, 0, 2),
            "tensor",
            tp_count,
            tensor_index,
        )

        hidden_out = (hidden_in.astype(f32) + summed + out_bias_full + shrink_bias_full).astype(bf16)
        start = tensor_index * local_rows
        standard_local = lax.dynamic_slice_in_dim(standard, start, local_rows, 0)
        inverse_local = lax.dynamic_slice_in_dim(inverse_std, start, local_rows, 0)
        input_grad = cotangent.astype(f32) + norm_backward(scaled, standard_local, inverse_local)
        return (
            hidden_out,
            input_grad,
            norm_grads[0],
            norm_grads[1],
            norm_grads[2],
            norm_grads[3],
            attend_weight_grad,
            attend_bias_out,
            output_weight_grad,
            out_bias_grad,
            expand_weight_grad,
            expand_bias_out,
            shrink_weight_grad,
            out_bias_grad,
        )
    in_specs = (
        P(("dp", "tensor"), None),
        P(("dp", "tensor"), None),
        P("dp", None),
        P("dp"),
        P(("dp", "tensor")),
        P(("dp", "tensor")),
        P(("dp", "tensor")),
        P(("dp", "tensor")),
        P("dp", None, "tensor"),
        P(None, ("tensor", "dp")),
        P("tensor", "dp"),
        P(("dp", "tensor")),
        P("dp", "tensor"),
        P(("tensor", "dp")),
        P("tensor", "dp"),
        P(("dp", "tensor")),
    )
    out_specs = (
        P(("dp", "tensor"), None),
        P(("dp", "tensor"), None),
        P(("dp", "tensor")),
        P(("dp", "tensor")),
        P(("dp", "tensor")),
        P(("dp", "tensor")),
        P("dp", None, "tensor"),
        P(None, ("tensor", "dp")),
        P("tensor", "dp"),
        P(("dp", "tensor")),
        P("dp", "tensor"),
        P(("tensor", "dp")),
        P("tensor", "dp"),
        P(("dp", "tensor")),
    )
    return jax.shard_map(
        per_device, mesh=mesh, in_specs=in_specs, out_specs=out_specs, check_vma=False
    )
```

```python
import jax
import jax.numpy as jnp
from jax import lax
from jax.sharding import PartitionSpec as P

HD = 64
ROT = 16


EPSILON = 1e-05
NEGATIVE = -1000000000.0


def rotate(tensor, cos_table, sin_table, rot_dims):
    half_dims = rot_dims // 2
    lower_half = tensor[..., :half_dims]
    upper_half = tensor[..., half_dims:rot_dims]
    return jnp.concatenate(
        [
            lower_half * cos_table - upper_half * sin_table,
            upper_half * cos_table + lower_half * sin_table,
            tensor[..., rot_dims:],
        ],
        axis=-1,
    )


def norm_backward(scaled, standard, inverse_std):
    mean_scaled = jnp.mean(scaled, axis=-1, keepdims=True)
    mean_cross = jnp.mean(scaled * standard, axis=-1, keepdims=True)
    return inverse_std * (scaled - mean_scaled - standard * mean_cross)


def lane_rows(parts, axis=1):
    padded = []
    for part in parts:
        extra = -part.shape[1] % 128
        padded.append(jnp.pad(part, ((0, 0), (0, extra))))
    joined = jnp.concatenate(padded, axis=axis)
    joined = joined.reshape(joined.shape[0], -1, 128)
    joined = jnp.pad(joined, ((0, 0), (0, -joined.shape[1] % 16), (0, 0)))
    return joined.reshape(-1, 128)


def gather_rows(parts, axis):
    flat, offsets, at = [], [], 0
    for part in parts:
        part = part.reshape(-1)
        extra = -part.shape[0] % 128
        flat.append(jnp.pad(part, (0, extra)))
        offsets.append(at)
        at += part.shape[0] + extra
    joined = jnp.concatenate(flat).reshape(-1, 128)
    joined = jnp.pad(joined, ((0, -joined.shape[0] % 16), (0, 0)))
    gathered = lax.all_gather(joined, axis, axis=0)
    return gathered.reshape(gathered.shape[0], -1), offsets


def ring_gather(block, axis, count, index):
    parts = [block] + [
        lax.ppermute(block, axis, [(j, (j + k) % count) for j in range(count)])
        for k in range(1, count)
    ]
    backward = jnp.stack([parts[0]] + parts[:0:-1])
    doubled = jnp.concatenate([backward, backward])
    return lax.dynamic_slice_in_dim(doubled, (count - index) % count, count, 0)


def ring_reduce(chunks, axis, count, index):
    total = lax.dynamic_index_in_dim(chunks, index, 0, keepdims=False).astype(jnp.float32)
    for k in range(1, count):
        send = lax.dynamic_index_in_dim(chunks, (index + k) % count, 0, keepdims=False)
        moved = lax.ppermute(send, axis, [(j, (j + k) % count) for j in range(count)])
        total = total + moved.astype(jnp.float32)
    return total


def ring_neighbour_steps(chunks, axis, order, index):
    count = len(order)
    position_of = [order.index(d) for d in range(count)]
    ahead = [(order[p], order[(p + 1) % count]) for p in range(count)]
    behind = [(order[p], order[(p - 1) % count]) for p in range(count)]
    half = chunks.shape[1] // 2
    by_ring = jnp.stack([chunks[order[q]] for q in range(count)])
    ring_a, ring_b = by_ring[:, :half], by_ring[:, half:]
    mine = jnp.asarray(position_of, jnp.int32)[index]

    def own(ring, at):
        return lax.dynamic_index_in_dim(ring, at % count, 0, keepdims=False).astype(jnp.float32)

    total_a = own(ring_a, mine - 1)
    total_b = own(ring_b, mine + 1)
    for step in range(1, count):
        moved_a = lax.ppermute(total_a.astype(chunks.dtype), axis, ahead)
        moved_b = lax.ppermute(total_b.astype(chunks.dtype), axis, behind)
        total_a = moved_a.astype(jnp.float32) + own(ring_a, mine - 1 - step)
        total_b = moved_b.astype(jnp.float32) + own(ring_b, mine + 1 + step)
        total_a, total_b = yield (total_a, total_b)
    yield jnp.concatenate([total_a, total_b], axis=0)


def solution(mesh):
    dp_count = mesh.shape["dp"]
    tp_count = mesh.shape["tensor"]

    def per_device(
        hidden_in,
        cotangent,
        segment_ids,
        live_count,
        first_gain,
        first_bias,
        second_gain,
        second_bias,
        attend_weight,
        attend_bias,
        output_weight,
        output_bias,
        expand_weight,
        expand_bias,
        shrink_weight,
        shrink_bias,
    ):
        f32 = jnp.float32
        bf16 = jnp.bfloat16
        local_rows, width = hidden_in.shape
        group_rows = local_rows * tp_count
        piece = first_gain.shape[0]
        dp_rows, _, local_cols = attend_weight.shape
        local_ff = expand_weight.shape[1]
        tensor_index = lax.axis_index("tensor")

        small = jnp.concatenate(
            [
                first_gain,
                first_bias,
                second_gain,
                second_bias,
                output_bias,
                shrink_bias,
                attend_bias.reshape(-1),
                expand_bias,
            ]
        )
        small_len = small.shape[0]
        gathered = ring_gather(
            jnp.concatenate([hidden_in, cotangent], axis=0), "tensor", tp_count, tensor_index
        )
        rows_all = gathered[:, :local_rows].reshape(group_rows, width)
        grad_rows = gathered[:, local_rows:].reshape(group_rows, width)

        attend_all, (attend_at, output_at, small_at) = gather_rows(
            [attend_weight, output_weight, small], "dp"
        )
        attend_full = attend_all[:, attend_at : attend_at + attend_weight.size].reshape(
            dp_count * dp_rows, 3, local_cols
        )
        output_parts = attend_all[:, output_at : output_at + output_weight.size].reshape(
            dp_count, local_cols, dp_rows
        )
        small_all = ring_gather(
            attend_all[:, small_at : small_at + small_len], "tensor", tp_count, tensor_index
        ).transpose(1, 0, 2)

        def full_vector(k):
            return small_all[:, :, k * piece : (k + 1) * piece].reshape(-1).astype(f32)

        gain_one, bias_one, gain_two, bias_two, out_bias_full, shrink_bias_full = [
            full_vector(k) for k in range(6)
        ]
        small_mine = lax.dynamic_index_in_dim(small_all, tensor_index, axis=1, keepdims=False)
        attend_bias_full = (
            small_mine[:, 6 * piece : 6 * piece + attend_bias.size]
            .reshape(dp_count, 3, attend_bias.shape[1])
            .transpose(1, 0, 2)
            .reshape(3, local_cols)
        )
        expand_bias_full = small_mine[:, 6 * piece + attend_bias.size :].reshape(-1)

        ffn_all, (expand_at, shrink_at) = gather_rows([expand_weight, shrink_weight], "dp")
        expand_full = ffn_all[:, expand_at : expand_at + expand_weight.size].reshape(
            dp_count * dp_rows, local_ff
        )
        shrink_parts = ffn_all[:, shrink_at : shrink_at + shrink_weight.size].reshape(
            dp_count, local_ff, dp_rows
        )

        local_heads = local_cols // HD
        scale = HD ** (-0.5)
        rows_float = rows_all.astype(f32)
        centre = rows_float - jnp.mean(rows_float, axis=-1, keepdims=True)
        inverse_std = lax.rsqrt(jnp.mean(centre * centre, axis=-1, keepdims=True) + EPSILON)
        standard = centre * inverse_std
        branch_one = (standard * gain_one + bias_one).astype(bf16)
        branch_two = (standard * gain_two + bias_two).astype(bf16)
        grad_rows_parts = grad_rows.reshape(group_rows, dp_count, dp_rows)

        projected = (
            jnp.einsum("td,dcn->tcn", branch_one, attend_full, preferred_element_type=f32)
            + attend_bias_full.astype(f32)[None]
        )
        segments = segment_ids[0]
        index = jnp.arange(group_rows)
        same_seq = segments[:, None] == segments[None, :]
        positions = jnp.sum((same_seq & (index[None, :] < index[:, None])).astype(f32), axis=1)
        allowed = (
            same_seq
            & (index[None, :] <= index[:, None])
            & ((index[None, :] < live_count[0]) | (index[None, :] == index[:, None]))
        )
        half_dims = ROT // 2
        inverse = 10000.0 ** (-jnp.arange(half_dims).astype(f32) * 2.0 / ROT)
        angles = positions[:, None] * inverse[None, :]
        cos_table = jnp.cos(angles)[:, None, :]
        sin_table = jnp.sin(angles)[:, None, :]
        per_head = projected.reshape(group_rows, 3, local_heads, HD)
        queries = rotate(per_head[:, 0], cos_table, sin_table, ROT).astype(bf16)
        keys_rot = rotate(per_head[:, 1], cos_table, sin_table, ROT).astype(bf16)
        values = per_head[:, 2].astype(bf16)
        scores = jnp.einsum("thd,uhd->htu", queries, keys_rot, preferred_element_type=f32) * scale
        scores = jnp.where(allowed[None], scores, NEGATIVE)
        top_score = jnp.max(scores, axis=-1, keepdims=True)
        log_total = top_score + jnp.log(jnp.sum(jnp.exp(scores - top_score), axis=-1, keepdims=True))
        probs = jnp.exp(scores - log_total)
        mixed = jnp.einsum("htu,uhd->thd", probs.astype(bf16), values, preferred_element_type=f32)
        mixed = mixed.reshape(group_rows, local_heads * HD).astype(bf16)
        attn_out = jnp.einsum(
            "tn,kne->tke", mixed, output_parts, preferred_element_type=f32
        ).reshape(group_rows, width)

        grad_mixed = jnp.einsum(
            "tke,kne->tn", grad_rows_parts, output_parts, preferred_element_type=f32
        ).astype(bf16)
        output_grad = jnp.einsum("tn,tke->kne", mixed, grad_rows_parts, preferred_element_type=f32)
        grad_mixed = grad_mixed.reshape(group_rows, local_heads, HD)
        probs_again = jnp.where(allowed[None], probs, 0.0)
        grad_values = jnp.einsum(
            "htu,thd->uhd", probs_again.astype(bf16), grad_mixed, preferred_element_type=f32
        )
        grad_probs = jnp.einsum("thd,uhd->htu", grad_mixed, values, preferred_element_type=f32)
        row_cross = jnp.sum(grad_probs * probs_again, axis=-1, keepdims=True)
        grad_scores = (probs_again * (grad_probs - row_cross)).astype(bf16)
        grad_queries = (
            jnp.einsum("htu,uhd->thd", grad_scores, keys_rot, preferred_element_type=f32) * scale
        )
        grad_keys = jnp.einsum("htu,thd->uhd", grad_scores, queries, preferred_element_type=f32) * scale
        grad_projected = jnp.stack(
            [
                rotate(grad_queries, cos_table, -sin_table, ROT),
                rotate(grad_keys, cos_table, -sin_table, ROT),
                grad_values,
            ],
            axis=1,
        )
        grad_projected = grad_projected.reshape(group_rows, 3, local_cols).astype(bf16)
        attend_bias_grad = jnp.sum(grad_projected.astype(f32), axis=0)
        attend_grad = jnp.einsum("td,tcn->dcn", branch_one, grad_projected, preferred_element_type=f32)
        grad_one = jnp.einsum("tcn,dcn->td", grad_projected, attend_full, preferred_element_type=f32)

        attend_bias_parts = (
            attend_bias_grad.reshape(3, dp_count, attend_bias.shape[1])
            .transpose(1, 0, 2)
            .reshape(dp_count, -1)
        )
        attn_payload = lane_rows(
            [attend_grad.reshape(dp_count, -1), output_grad.reshape(dp_count, -1), attend_bias_parts],
            axis=1,
        ).astype(bf16)
        expand_full, shrink_parts, _ = lax.optimization_barrier(
            (expand_full, shrink_parts, attn_payload)
        )

        use_ring = dp_count == 8
        if use_ring:
            ring = ring_neighbour_steps(
                attn_payload.reshape(dp_count, -1, 128),
                "dp",
                (0, 2, 4, 6, 7, 5, 3, 1),
                lax.axis_index("dp"),
            )
            ring_state = ring.send(next(ring))

        expanded = jnp.dot(
            branch_two, expand_full, preferred_element_type=f32
        ) + expand_bias_full.astype(f32)
        if use_ring:
            ring_state, expanded = lax.optimization_barrier((ring_state, expanded))
            for _ in range(3):
                ring_state = ring.send(ring_state)
        activated, gelu_back = jax.vjp(lambda value: jax.nn.gelu(value, approximate=False), expanded)
        activated_low = activated.astype(bf16)
        ffn_out = jnp.einsum(
            "tf,kfe->tke", activated_low, shrink_parts, preferred_element_type=f32
        ).reshape(group_rows, width)
        grad_activated = jnp.einsum(
            "tke,kfe->tf", grad_rows_parts, shrink_parts, preferred_element_type=f32
        )
        if use_ring:
            ring_state, grad_activated = lax.optimization_barrier((ring_state, grad_activated))
            for _ in range(3):
                ring_state = ring.send(ring_state)
        shrink_grad = jnp.einsum(
            "tf,tke->kfe", activated_low, grad_rows_parts, preferred_element_type=f32
        )
        grad_expanded = gelu_back(grad_activated)[0].astype(bf16)
        expand_bias_grad = jnp.sum(grad_expanded.astype(f32), axis=0)
        expand_grad = jnp.einsum("td,tf->df", branch_two, grad_expanded, preferred_element_type=f32)
        grad_two = jnp.einsum("tf,df->td", grad_expanded, expand_full, preferred_element_type=f32)
        out_bias_sum = jnp.sum(grad_rows.astype(f32), axis=0).reshape(dp_count, tp_count, piece)
        out_bias_mine = lax.dynamic_index_in_dim(out_bias_sum, tensor_index, axis=1, keepdims=False)

        partial_out = ffn_out + attn_out

        norm_partials = jnp.stack(
            [
                jnp.sum(grad_one * standard, axis=0),
                jnp.sum(grad_one, axis=0),
                jnp.sum(grad_two * standard, axis=0),
                jnp.sum(grad_two, axis=0),
            ]
        )
        scaled_parts = grad_one * gain_one + grad_two * gain_two
        token_parts = jnp.concatenate([partial_out, scaled_parts], axis=1).reshape(
            tp_count, local_rows, 2 * width
        )
        reduced = ring_reduce(token_parts.astype(bf16), "tensor", tp_count, tensor_index)
        summed = reduced[:, :width]
        scaled = reduced[:, width:]
        if use_ring:
            attn_reduced = ring_state
        else:
            attn_reduced = lax.psum_scatter(attn_payload, "dp", scatter_dimension=0, tiled=True)
        ffn_payload = lane_rows(
            [
                expand_grad.reshape(dp_count, -1),
                shrink_grad.reshape(dp_count, -1),
                expand_bias_grad.reshape(dp_count, -1),
                out_bias_mine,
                norm_partials.reshape(4, dp_count, -1).transpose(1, 0, 2).reshape(dp_count, -1),
            ],
            axis=1,
        ).astype(bf16)
        attn_grads = attn_reduced.reshape(-1).astype(f32)
        at = 0
        attend_weight_grad = attn_grads[at : at + attend_weight.size].reshape(attend_weight.shape)
        at += -(-attend_weight.size // 128) * 128
        output_weight_grad = attn_grads[at : at + output_weight.size].reshape(output_weight.shape)
        at += -(-output_weight.size // 128) * 128
        attend_bias_out = attn_grads[at : at + attend_bias.size].reshape(attend_bias.shape)


        ffn_grads = lax.psum_scatter(
            ffn_payload,
            "dp",
            scatter_dimension=0,
            tiled=True,
        ).reshape(-1).astype(f32)
        at = 0
        expand_weight_grad = ffn_grads[at : at + expand_weight.size].reshape(expand_weight.shape)
        at += -(-expand_weight.size // 128) * 128
        shrink_weight_grad = ffn_grads[at : at + shrink_weight.size].reshape(shrink_weight.shape)
        at += -(-shrink_weight.size // 128) * 128
        expand_bias_out = ffn_grads[at : at + expand_bias.size]
        at += -(-expand_bias.size // 128) * 128
        out_bias_grad = ffn_grads[at : at + piece]
        at += -(-piece // 128) * 128
        norm_grads = ring_reduce(
            ffn_grads[at : at + 4 * tp_count * piece].reshape(4, tp_count, piece).transpose(1, 0, 2),
            "tensor",
            tp_count,
            tensor_index,
        )

        hidden_out = (hidden_in.astype(f32) + summed + out_bias_full + shrink_bias_full).astype(bf16)
        start = tensor_index * local_rows
        standard_local = lax.dynamic_slice_in_dim(standard, start, local_rows, 0)
        inverse_local = lax.dynamic_slice_in_dim(inverse_std, start, local_rows, 0)
        input_grad = cotangent.astype(f32) + norm_backward(scaled, standard_local, inverse_local)
        return (
            hidden_out,
            input_grad,
            norm_grads[0],
            norm_grads[1],
            norm_grads[2],
            norm_grads[3],
            attend_weight_grad,
            attend_bias_out,
            output_weight_grad,
            out_bias_grad,
            expand_weight_grad,
            expand_bias_out,
            shrink_weight_grad,
            out_bias_grad,
        )
    in_specs = (
        P(("dp", "tensor"), None),
        P(("dp", "tensor"), None),
        P("dp", None),
        P("dp"),
        P(("dp", "tensor")),
        P(("dp", "tensor")),
        P(("dp", "tensor")),
        P(("dp", "tensor")),
        P("dp", None, "tensor"),
        P(None, ("tensor", "dp")),
        P("tensor", "dp"),
        P(("dp", "tensor")),
        P("dp", "tensor"),
        P(("tensor", "dp")),
        P("tensor", "dp"),
        P(("dp", "tensor")),
    )
    out_specs = (
        P(("dp", "tensor"), None),
        P(("dp", "tensor"), None),
        P(("dp", "tensor")),
        P(("dp", "tensor")),
        P(("dp", "tensor")),
        P(("dp", "tensor")),
        P("dp", None, "tensor"),
        P(None, ("tensor", "dp")),
        P("tensor", "dp"),
        P(("dp", "tensor")),
        P("dp", "tensor"),
        P(("tensor", "dp")),
        P("tensor", "dp"),
        P(("dp", "tensor")),
    )
    return jax.shard_map(
        per_device, mesh=mesh, in_specs=in_specs, out_specs=out_specs, check_vma=False
    )
```
